32 devices in a mesh: grp: 2 (over x), slab: 16 (over z, y, core).
Axes of the slice: x: 2, y: 2, z: 4, core: 2. Of those that a mesh axis runs over, the one named last changes fastest.
Arguments:
- volume: bfloat16 [32, 64, 16, 256], P(None, ('grp', 'slab')), parts along dimension 1, may hold values from -6 to 6
- weight_one: bfloat16 [27, 32, 32], replicated, may hold values from -0.21875 to 0.21875
- weight_two: bfloat16 [27, 32, 32], replicated, may hold values from -0.21875 to 0.21875
- cotangent: bfloat16 [32, 32, 8, 128], P(None, ('grp', 'slab')), parts along dimension 1, may hold values from -6 to 6
Outputs:
- output: bfloat16 [32, 32, 8, 128], P(None, ('grp', 'slab')), parts along dimension 1
- grad_volume: bfloat16 [32, 64, 16, 256], P(None, ('grp', 'slab')), parts along dimension 1
- grad_one: float32 [54, 32, 32], P('grp'), parts along dimension 0
- grad_two: float32 [54, 32, 32], P('grp'), parts along dimension 0
The draws below stay inside these ranges and needn't reach their ends.
There are 2 independent parts, one for each index of `grp`. The reference program is written for one: setup_inputs(seed, part) draws one part's arguments, and reference() takes and returns one part's arrays. A program takes and returns all parts, laid end to end along the dimension named above; an argument that names none is the same for every part. Nothing has to cross between parts.
All inputs are finite; a program needn't handle non-finite values.
Results may differ from the reference program's by a relative error of at most 0.0051.
Values may be sent and summed in bfloat16 or wider, within the bound.
No kernel may reach another device: no remote copies, remote signals or barrier semaphores. Data moves between devices by JAX's collectives and lax.ppermute only.
A program may use at most 64 MiB of HBM per device.

```python
import jax
import jax.numpy as jnp
from jax import lax

C = 32
HH = 16
W = 256
D = 32


def shard_levels(own_key, extent, cuts, low, top_value):
    level = 1.0
    for axis_at, parts in cuts:
        heights = jax.random.uniform(jax.random.fold_in(jax.random.fold_in(own_key, 6), axis_at), (parts,), jnp.float32, low / len(cuts), top_value / len(cuts))
        level = level * jnp.repeat(jnp.exp(heights), extent[axis_at] // parts).reshape((-1,) + (1,) * (len(extent) - 1 - axis_at))
    return level


def bell_draw(stream_key, shape, width, reach, cuts=(), held_as=jnp.bfloat16):
    factor_of = shard_levels(stream_key, shape, cuts, -0.22, 0.18) if cuts else 1.0
    drawn = jax.random.normal(stream_key, shape, jnp.float32) * width * factor_of
    return jnp.minimum(jnp.maximum(drawn, -reach), reach).astype(held_as)


def setup_inputs(seed: int = 0, part: int = 0) -> dict:
    arg_keys = jax.random.split(jax.random.key(seed), 5)
    part_splits = jax.random.split(jax.random.fold_in(arg_keys[4], part), 5)
    return {
        "volume": bell_draw(part_splits[0], (C, D, HH, W), 1.0, 6.0, ((1, 16),)),
        "weight_one": bell_draw(arg_keys[1], (27, C, C), (27 * C) ** -0.5, 0.21875),
        "weight_two": bell_draw(arg_keys[2], (27, C, C), (27 * C) ** -0.5, 0.21875),
        "cotangent": bell_draw(part_splits[3], (C, D // 2, HH // 2, W // 2), 1.0, 6.0, ((1, 16),)),
    }


def convolve(field, weights, stride):
    size = weights.shape[1]
    kernel = weights.reshape(3, 3, 3, size, size).transpose(3, 4, 0, 1, 2)
    result = lax.conv_general_dilated(field[None], kernel, (stride, stride, stride), [(1, 1), (1, 1), (1, 1)], dimension_numbers=('NCDHW', 'OIDHW', 'NCDHW'), precision=lax.Precision.HIGHEST)
    return result[0]

def reference(volume, weight_one, weight_two, cotangent):
    volume_wide = volume.astype(jnp.float32)
    first_weights = weight_one.astype(jnp.float32)
    preact = convolve(volume_wide, first_weights, 1)
    hidden = lax.optimization_barrier(jax.nn.silu(preact).astype(jnp.bfloat16))
    hidden_wide = hidden.astype(jnp.float32)
    output, back_two = jax.vjp(lambda field, weights: convolve(field, weights, 2), hidden_wide, weight_two.astype(jnp.float32))
    grad_hidden, grad_two = back_two(cotangent.astype(jnp.float32))
    sigma = jax.nn.sigmoid(preact)
    grad_pre = lax.optimization_barrier((grad_hidden * (sigma * (1.0 + preact * (1.0 - sigma)))).astype(jnp.bfloat16))
    unused, back_one = jax.vjp(lambda field, weights: convolve(field, weights, 1), volume_wide, first_weights)
    grad_volume, grad_one = back_one(grad_pre.astype(jnp.float32))
    return (output.astype(jnp.bfloat16), grad_volume.astype(jnp.bfloat16), grad_one, grad_two)
```

```python
import jax
import jax.numpy as jnp
from jax import lax
from jax.sharding import PartitionSpec as P


def extended_2(shard, sides, width):
    for axis, dim in sides:
        devices, length = (lax.axis_size(axis), shard.shape[dim])
        up = [(i, (i + 1) % devices) for i in range(devices - 1)]
        down = [(j, i) for i, j in up]
        last = lax.slice_in_dim(shard, length - width, length, axis=dim)
        initial = lax.slice_in_dim(shard, 0, width, axis=dim)
        before = lax.ppermute(last, axis, up)
        after = lax.ppermute(initial, axis, down)
        shard = jnp.concatenate([before, shard, after], axis=dim)
    return shard


def passed_along(block, axis, distance):
    devices = range(lax.axis_size(axis))
    route = [(i - distance, i) for i in devices if i - distance in devices]
    return lax.ppermute(block, axis, route)


def pad_sides(field):
    return jnp.pad(field, ((0, 0), (0, 0), (1, 1), (1, 1)))


def column_stack(field, stride, count, start):
    pieces = []
    for along_cols in range(3):
        first = start(along_cols)
        pieces.append(field[..., first : first + stride * (count - 1) + 1 : stride])
    return jnp.concatenate(pieces, 0)


def summed_over(terms, axis):
    devices = lax.axis_size(axis)
    flat = terms.reshape(-1)
    room = -flat.shape[0] % devices
    flat = jnp.pad(flat, (0, room)).reshape(devices, -1)
    mine = lax.all_to_all(flat, axis, 0, 0, tiled=True).sum(0, keepdims=True)
    whole = lax.all_to_all(jnp.broadcast_to(mine, flat.shape), axis, 0, 0, tiled=True)
    return whole.reshape(-1)[: terms.size].reshape(terms.shape)


def forward_kernel(weights):
    size = weights.shape[1]
    return (
        weights.reshape(3, 3, 3, size, size).transpose(0, 1, 3, 2, 4).reshape(3, 3, size, 3 * size)
    )


def backward_kernel(weights):
    size = weights.shape[1]
    return weights.reshape(3, 3, 3 * size, size)


def fold_term(term):
    size = term.shape[0]
    return term.reshape(size, 3, size).transpose(1, 0, 2)


def gather_terms(listed):
    stacked = jnp.stack(listed)
    return stacked.reshape(27, stacked.shape[2], stacked.shape[3])


def on_device(volume, weight_one, weight_two, cotangent):
    channels, planes, height, columns = volume.shape
    half_planes = planes // 2
    half_rows = height // 2
    half_cols = columns // 2
    front_one = forward_kernel(weight_one)
    front_two = forward_kernel(weight_two)
    rear_one = backward_kernel(weight_one)
    padded = pad_sides(extended_2(volume, (("slab", 1),), 1))
    volume_cols = column_stack(padded, 1, columns, lambda along_cols: along_cols)
    preact = jnp.zeros((channels, planes, height, columns), jnp.float32)
    for along_depth in range(3):
        for along_rows in range(3):
            window = volume_cols[
                :, along_depth : along_depth + planes, along_rows : along_rows + height, :
            ]
            preact = preact + jnp.einsum(
                "ok,kdhw->odhw",
                front_one[along_depth, along_rows],
                window,
                preferred_element_type=jnp.float32,
            )
    hidden = jax.nn.silu(preact).astype(jnp.bfloat16)
    upper_plane = passed_along(cotangent, "slab", -1)
    lower_plane = passed_along(hidden[:, planes - 1 :], "slab", 1)
    stacked = jnp.concatenate([lower_plane, hidden], 1)
    stacked = jnp.pad(stacked, ((0, 0), (0, 0), (1, 1), (0, 0)))
    picks = jnp.arange(columns)[:, None, None] == (
        2 * jnp.arange(half_cols)[None, None, :] + jnp.arange(3)[None, :, None] - 1
    )
    hidden_cols = jnp.einsum(
        "qdhp,pck->cqdhk", stacked, picks.astype(jnp.bfloat16), preferred_element_type=jnp.float32
    )
    hidden_cols = hidden_cols.astype(jnp.bfloat16).reshape(
        3 * channels, planes + 1, height + 2, half_cols
    )
    output = jnp.zeros((channels, half_planes, half_rows, half_cols), jnp.float32)
    terms_two = []
    for along_depth in range(3):
        for along_rows in range(3):
            window = hidden_cols[
                :,
                along_depth : along_depth + planes - 1 : 2,
                along_rows : along_rows + height - 1 : 2,
                :,
            ]
            output = output + jnp.einsum(
                "ok,kdhw->odhw",
                front_two[along_depth, along_rows],
                window,
                preferred_element_type=jnp.float32,
            )
            terms_two.append(
                fold_term(
                    jnp.einsum(
                        "odhw,kdhw->ok", cotangent, window, preferred_element_type=jnp.float32
                    )
                )
            )
    extended = jnp.concatenate([cotangent, upper_plane], 1)
    extended = jnp.pad(extended, ((0, 0), (0, 0), (0, 1), (0, 1)))
    parity_taps = [[(1, 0)], [(2, 0), (0, 1)]]
    classes = []
    for depth_parity in range(2):
        for row_parity in range(2):
            for col_parity in range(2):
                pieces = []
                kernels = []
                for tap_depth, skip_depth in parity_taps[depth_parity]:
                    for tap_row, skip_row in parity_taps[row_parity]:
                        for tap_col, skip_col in parity_taps[col_parity]:
                            pieces.append(
                                extended[
                                    :,
                                    skip_depth : skip_depth + half_planes,
                                    skip_row : skip_row + half_rows,
                                    skip_col : skip_col + half_cols,
                                ]
                            )
                            kernels.append(weight_two[9 * tap_depth + 3 * tap_row + tap_col])
                joined = jnp.concatenate(pieces, 0)
                joined_kernel = jnp.concatenate(kernels, 0)
                classes.append(
                    jnp.einsum(
                        "kq,kdhw->qdhw", joined_kernel, joined, preferred_element_type=jnp.float32
                    )
                )
    parity_grid = jnp.stack(classes).reshape(2, 2, 2, channels, half_planes, half_rows, half_cols)
    grad_hidden = parity_grid.transpose(3, 4, 0, 5, 1, 6, 2).reshape(
        channels, planes, height, columns
    )
    sigma = jax.nn.sigmoid(preact)
    grad_pre = (grad_hidden * (sigma * (1.0 + preact * (1.0 - sigma)))).astype(jnp.bfloat16)
    rimmed = pad_sides(extended_2(grad_pre, (("slab", 1),), 1))
    rimmed_cols = column_stack(rimmed, 1, columns, lambda along_cols: 2 - along_cols)
    grad_volume = jnp.zeros((channels, planes, height, columns), jnp.float32)
    terms_one = []
    for along_depth in range(3):
        for along_rows in range(3):
            window = volume_cols[
                :, along_depth : along_depth + planes, along_rows : along_rows + height, :
            ]
            terms_one.append(
                fold_term(
                    jnp.einsum(
                        "odhw,kdhw->ok", grad_pre, window, preferred_element_type=jnp.float32
                    )
                )
            )
            back_window = rimmed_cols[
                :,
                2 - along_depth : 2 - along_depth + planes,
                2 - along_rows : 2 - along_rows + height,
                :,
            ]
            grad_volume = grad_volume + jnp.einsum(
                "kq,kdhw->qdhw",
                rear_one[along_depth, along_rows],
                back_window,
                preferred_element_type=jnp.float32,
            )
    grad_one, grad_two = summed_over(
        jnp.stack([gather_terms(terms_one), gather_terms(terms_two)]), "slab"
    )
    return (output.astype(jnp.bfloat16), grad_volume.astype(jnp.bfloat16), grad_one, grad_two)


def solution(mesh):
    in_specs = (
        P(None, ("grp", "slab"), None, None),
        P(),
        P(),
        P(None, ("grp", "slab"), None, None),
    )
    out_specs = (
        P(None, ("grp", "slab"), None, None),
        P(None, ("grp", "slab"), None, None),
        P("grp", None, None),
        P("grp", None, None),
    )
    return jax.shard_map(
        on_device, mesh=mesh, in_specs=in_specs, out_specs=out_specs, check_vma=False
    )
```

```python
import jax
import numpy as np
import jax.numpy as jnp
from jax import lax
from jax.sharding import PartitionSpec as P


def extended_2(shard, sides, width):
    for axis, dim in sides:
        devices, length = (lax.axis_size(axis), shard.shape[dim])
        up = [(i, (i + 1) % devices) for i in range(devices - 1)]
        down = [(j, i) for i, j in up]
        last = lax.slice_in_dim(shard, length - width, length, axis=dim)
        initial = lax.slice_in_dim(shard, 0, width, axis=dim)
        before = lax.ppermute(last, axis, up)
        after = lax.ppermute(initial, axis, down)
        shard = jnp.concatenate([before, shard, after], axis=dim)
    return shard


def passed_along(block, axis, distance):
    devices = range(lax.axis_size(axis))
    route = [(i - distance, i) for i in devices if i - distance in devices]
    return lax.ppermute(block, axis, route)


def pad_sides(field):
    return jnp.pad(field, ((0, 0), (0, 0), (1, 1), (1, 1)))


def column_stack(field, stride, count, start):
    pieces = []
    for along_cols in range(3):
        first = start(along_cols)
        pieces.append(field[..., first : first + stride * (count - 1) + 1 : stride])
    return jnp.concatenate(pieces, 0)


def summed_over(terms, axis):
    devices = lax.axis_size(axis)
    flat = terms.reshape(-1)
    room = -flat.shape[0] % devices
    flat = jnp.pad(flat, (0, room)).reshape(devices, -1)
    mine = lax.all_to_all(flat, axis, 0, 0, tiled=True).sum(0, keepdims=True)
    whole = lax.all_to_all(jnp.broadcast_to(mine, flat.shape), axis, 0, 0, tiled=True)
    return whole.reshape(-1)[: terms.size].reshape(terms.shape)


def forward_kernel(weights):
    size = weights.shape[1]
    return (
        weights.reshape(3, 3, 3, size, size).transpose(0, 1, 3, 2, 4).reshape(3, 3, size, 3 * size)
    )


def backward_kernel(weights):
    size = weights.shape[1]
    return weights.reshape(3, 3, 3 * size, size)


def fold_term(term):
    size = term.shape[0]
    return term.reshape(size, 3, size).transpose(1, 0, 2)


def fold_terms(summed):
    size = summed.shape[2]
    folded = summed.reshape(2, 9, size, 3, size).transpose(0, 1, 3, 2, 4)
    folded = folded.reshape(2, 27, size, size)
    return folded[0], folded[1]


def gather_terms(listed):
    stacked = jnp.stack(listed)
    return stacked.reshape(27, stacked.shape[2], stacked.shape[3])


def on_device(volume, weight_one, weight_two, cotangent):
    channels, planes, height, columns = volume.shape
    half_planes = planes // 2
    half_rows = height // 2
    half_cols = columns // 2
    front_one = forward_kernel(weight_one)
    front_two = forward_kernel(weight_two)
    rear_one = backward_kernel(weight_one).transpose(0, 1, 3, 2)
    padded = pad_sides(extended_2(volume, (("slab", 1),), 1))
    volume_cols = column_stack(padded, 1, columns, lambda along_cols: along_cols)
    preact = jnp.zeros((channels, planes, height, columns), jnp.float32)
    for along_depth in range(3):
        for along_rows in range(3):
            window = volume_cols[
                :, along_depth : along_depth + planes, along_rows : along_rows + height, :
            ]
            preact = preact + jnp.einsum(
                "ok,kdhw->odhw",
                front_one[along_depth, along_rows],
                window,
                preferred_element_type=jnp.float32,
            )
    hidden = jax.nn.silu(preact).astype(jnp.bfloat16)
    upper_plane = passed_along(cotangent, "slab", -1)
    lower_plane = passed_along(hidden[:, planes - 1 :], "slab", 1)
    stacked = jnp.concatenate([lower_plane, hidden], 1)
    stacked = jnp.pad(stacked, ((0, 0), (0, 0), (1, 1), (0, 0)))
    picks = jnp.arange(columns)[:, None, None] == (
        2 * jnp.arange(half_cols)[None, None, :] + jnp.arange(3)[None, :, None] - 1
    )
    hidden_cols = jnp.einsum(
        "qdhp,pck->cqdhk", stacked, picks.astype(jnp.bfloat16), preferred_element_type=jnp.float32
    )
    hidden_cols = hidden_cols.astype(jnp.bfloat16).reshape(
        3 * channels, planes + 1, height + 2, half_cols
    )
    output = jnp.zeros((channels, half_planes, half_rows, half_cols), jnp.float32)
    terms_two = []
    for along_depth in range(3):
        for along_rows in range(3):
            window = hidden_cols[
                :,
                along_depth : along_depth + planes - 1 : 2,
                along_rows : along_rows + height - 1 : 2,
                :,
            ]
            output = output + jnp.einsum(
                "ok,kdhw->odhw",
                front_two[along_depth, along_rows],
                window,
                preferred_element_type=jnp.float32,
            )
            terms_two.append(
                jnp.einsum("odhw,kdhw->ok", cotangent, window, preferred_element_type=jnp.float32)
            )
    extended = jnp.concatenate([cotangent, upper_plane], 1)
    extended = jnp.pad(extended, ((0, 0), (0, 0), (0, 1), (0, 1)))
    parity_taps = [[(1, 0)], [(2, 0), (0, 1)]]
    order = []
    for depth_parity in range(2):
        for row_parity in range(2):
            for col_parity in range(2):
                for tap_depth, _ in parity_taps[depth_parity]:
                    for tap_row, _ in parity_taps[row_parity]:
                        for tap_col, _ in parity_taps[col_parity]:
                            order.append(9 * tap_depth + 3 * tap_row + tap_col)
    ordered_two = weight_two[np.array(order)]
    taken = 0
    classes = []
    for depth_parity in range(2):
        for row_parity in range(2):
            for col_parity in range(2):
                pieces = []
                for tap_depth, skip_depth in parity_taps[depth_parity]:
                    for tap_row, skip_row in parity_taps[row_parity]:
                        for tap_col, skip_col in parity_taps[col_parity]:
                            pieces.append(
                                extended[
                                    :,
                                    skip_depth : skip_depth + half_planes,
                                    skip_row : skip_row + half_rows,
                                    skip_col : skip_col + half_cols,
                                ]
                            )
                joined = jnp.concatenate(pieces, 0)
                joined_kernel = ordered_two[taken : taken + len(pieces)].reshape(-1, channels)
                taken += len(pieces)
                classes.append(
                    jnp.einsum(
                        "kq,kdhw->qdhw", joined_kernel, joined, preferred_element_type=jnp.float32
                    )
                )
    parity_grid = jnp.stack(classes).reshape(2, 2, 2, channels, half_planes, half_rows, half_cols)
    grad_hidden = parity_grid.transpose(3, 4, 0, 5, 1, 6, 2).reshape(
        channels, planes, height, columns
    )
    sigma = jax.nn.sigmoid(preact)
    grad_pre = (grad_hidden * (sigma * (1.0 + preact * (1.0 - sigma)))).astype(jnp.bfloat16)
    rimmed = pad_sides(extended_2(grad_pre, (("slab", 1),), 1))
    rimmed_cols = column_stack(rimmed, 1, columns, lambda along_cols: 2 - along_cols)
    grad_volume = jnp.zeros((channels, planes, height, columns), jnp.float32)
    terms_one = []
    for along_depth in range(3):
        for along_rows in range(3):
            window = volume_cols[
                :, along_depth : along_depth + planes, along_rows : along_rows + height, :
            ]
            terms_one.append(
                jnp.einsum("odhw,kdhw->ok", grad_pre, window, preferred_element_type=jnp.float32)
            )
            back_window = rimmed_cols[
                :,
                2 - along_depth : 2 - along_depth + planes,
                2 - along_rows : 2 - along_rows + height,
                :,
            ]
            grad_volume = grad_volume + jnp.einsum(
                "qk,kdhw->qdhw",
                rear_one[along_depth, along_rows],
                back_window,
                preferred_element_type=jnp.float32,
            )
    summed = summed_over(jnp.stack([jnp.stack(terms_one), jnp.stack(terms_two)]), "slab")
    grad_one, grad_two = fold_terms(summed)
    return (output.astype(jnp.bfloat16), grad_volume.astype(jnp.bfloat16), grad_one, grad_two)


def solution(mesh):
    in_specs = (
        P(None, ("grp", "slab"), None, None),
        P(),
        P(),
        P(None, ("grp", "slab"), None, None),
    )
    out_specs = (
        P(None, ("grp", "slab"), None, None),
        P(None, ("grp", "slab"), None, None),
        P("grp", None, None),
        P("grp", None, None),
    )
    return jax.shard_map(
        on_device, mesh=mesh, in_specs=in_specs, out_specs=out_specs, check_vma=False
    )
```

```python
import jax
import numpy as np
import jax.numpy as jnp
from jax import lax
from jax.sharding import PartitionSpec as P


def extended_2(shard, sides, width):
    for axis, dim in sides:
        devices, length = (lax.axis_size(axis), shard.shape[dim])
        up = [(i, (i + 1) % devices) for i in range(devices - 1)]
        down = [(j, i) for i, j in up]
        last = lax.slice_in_dim(shard, length - width, length, axis=dim)
        initial = lax.slice_in_dim(shard, 0, width, axis=dim)
        before = lax.ppermute(last, axis, up)
        after = lax.ppermute(initial, axis, down)
        shard = jnp.concatenate([before, shard, after], axis=dim)
    return shard


def passed_along(block, axis, distance):
    devices = range(lax.axis_size(axis))
    route = [(i - distance, i) for i in devices if i - distance in devices]
    return lax.ppermute(block, axis, route)


def pad_sides(field):
    return jnp.pad(field, ((0, 0), (0, 0), (1, 1), (1, 1)))


def column_stack(field, stride, count, start):
    pieces = []
    for along_cols in range(3):
        first = start(along_cols)
        pieces.append(field[..., first : first + stride * (count - 1) + 1 : stride])
    return jnp.concatenate(pieces, 0)


def summed_over(terms, axis):
    devices = lax.axis_size(axis)
    flat = terms.reshape(-1)
    room = -flat.shape[0] % devices
    flat = jnp.pad(flat, (0, room)).reshape(devices, -1)
    mine = lax.all_to_all(flat, axis, 0, 0, tiled=True).sum(0, keepdims=True)
    whole = lax.all_to_all(jnp.broadcast_to(mine, flat.shape), axis, 0, 0, tiled=True)
    return whole.reshape(-1)[: terms.size].reshape(terms.shape)


def forward_kernel(weights):
    size = weights.shape[1]
    return (
        weights.reshape(3, 3, 3, size, size).transpose(0, 1, 3, 2, 4).reshape(3, 3, size, 3 * size)
    )


def backward_kernel(weights):
    size = weights.shape[1]
    return weights.reshape(3, 3, 3 * size, size)


def fold_term(term):
    size = term.shape[0]
    return term.reshape(size, 3, size).transpose(1, 0, 2)


def fold_terms(summed):
    size = summed.shape[2]
    folded = summed.reshape(2, 9, size, 3, size).transpose(0, 1, 3, 2, 4)
    folded = folded.reshape(2, 27, size, size)
    return folded[0], folded[1]


def gather_terms(listed):
    stacked = jnp.stack(listed)
    return stacked.reshape(27, stacked.shape[2], stacked.shape[3])


def on_device(volume, weight_one, weight_two, cotangent):
    channels, planes, height, columns = volume.shape
    half_planes = planes // 2
    half_rows = height // 2
    half_cols = columns // 2
    front_one = forward_kernel(weight_one)
    front_two = forward_kernel(weight_two)
    rear_one = backward_kernel(weight_one).transpose(0, 1, 3, 2)
    padded = pad_sides(extended_2(volume, (("slab", 1),), 2))
    volume_cols = column_stack(padded, 1, columns, lambda along_cols: along_cols)
    cot_ext = extended_2(cotangent, (("slab", 1),), 1)
    devices = lax.axis_size("slab")
    place = lax.axis_index("slab") * planes + jnp.arange(-1, planes + 1)
    inside = ((place >= 0) & (place < devices * planes))[None, :, None, None]
    preact = jnp.zeros((channels, planes + 2, height, columns), jnp.float32)
    for along_depth in range(3):
        for along_rows in range(3):
            window = volume_cols[
                :, along_depth : along_depth + planes + 2, along_rows : along_rows + height, :
            ]
            preact = preact + jnp.einsum(
                "ok,kdhw->odhw",
                front_one[along_depth, along_rows],
                window,
                preferred_element_type=jnp.float32,
            )
    hidden = jnp.where(inside, jax.nn.silu(preact), 0.0).astype(jnp.bfloat16)
    stacked = hidden[:, : planes + 1]
    stacked = jnp.pad(stacked, ((0, 0), (0, 0), (1, 1), (0, 0)))
    picks = jnp.arange(columns)[:, None, None] == (
        2 * jnp.arange(half_cols)[None, None, :] + jnp.arange(3)[None, :, None] - 1
    )
    hidden_cols = jnp.einsum(
        "qdhp,pck->cqdhk", stacked, picks.astype(jnp.bfloat16), preferred_element_type=jnp.float32
    )
    hidden_cols = hidden_cols.astype(jnp.bfloat16).reshape(
        3 * channels, planes + 1, height + 2, half_cols
    )
    output = jnp.zeros((channels, half_planes, half_rows, half_cols), jnp.float32)
    terms_two = []
    for along_depth in range(3):
        for along_rows in range(3):
            window = hidden_cols[
                :,
                along_depth : along_depth + planes - 1 : 2,
                along_rows : along_rows + height - 1 : 2,
                :,
            ]
            output = output + jnp.einsum(
                "ok,kdhw->odhw",
                front_two[along_depth, along_rows],
                window,
                preferred_element_type=jnp.float32,
            )
            terms_two.append(
                jnp.einsum("odhw,kdhw->ok", cotangent, window, preferred_element_type=jnp.float32)
            )
    extended = jnp.pad(cot_ext, ((0, 0), (0, 1), (0, 1), (0, 1)))
    class_planes = half_planes + 2
    parity_taps = [[(1, 0)], [(2, 0), (0, 1)]]
    order = []
    for depth_parity in range(2):
        for row_parity in range(2):
            for col_parity in range(2):
                for tap_depth, _ in parity_taps[depth_parity]:
                    for tap_row, _ in parity_taps[row_parity]:
                        for tap_col, _ in parity_taps[col_parity]:
                            order.append(9 * tap_depth + 3 * tap_row + tap_col)
    ordered_two = weight_two[np.array(order)]
    taken = 0
    classes = []
    for depth_parity in range(2):
        for row_parity in range(2):
            for col_parity in range(2):
                pieces = []
                for tap_depth, skip_depth in parity_taps[depth_parity]:
                    for tap_row, skip_row in parity_taps[row_parity]:
                        for tap_col, skip_col in parity_taps[col_parity]:
                            pieces.append(
                                extended[
                                    :,
                                    skip_depth : skip_depth + class_planes,
                                    skip_row : skip_row + half_rows,
                                    skip_col : skip_col + half_cols,
                                ]
                            )
                joined = jnp.concatenate(pieces, 0)
                joined_kernel = ordered_two[taken : taken + len(pieces)].reshape(-1, channels)
                taken += len(pieces)
                classes.append(
                    jnp.einsum(
                        "kq,kdhw->qdhw", joined_kernel, joined, preferred_element_type=jnp.float32
                    )
                )
    parity_grid = jnp.stack(classes).reshape(2, 2, 2, channels, class_planes, half_rows, half_cols)
    grad_hidden = parity_grid.transpose(3, 4, 0, 5, 1, 6, 2).reshape(
        channels, 2 * class_planes, height, columns
    )[:, 1 : planes + 3]
    sigma = jax.nn.sigmoid(preact)
    grad_rim = grad_hidden * (sigma * (1.0 + preact * (1.0 - sigma)))
    grad_rim = jnp.where(inside, grad_rim, 0.0).astype(jnp.bfloat16)
    grad_pre = grad_rim[:, 1 : planes + 1]
    rimmed = pad_sides(grad_rim)
    rimmed_cols = column_stack(rimmed, 1, columns, lambda along_cols: 2 - along_cols)
    grad_volume = jnp.zeros((channels, planes, height, columns), jnp.float32)
    terms_one = []
    for along_depth in range(3):
        for along_rows in range(3):
            window = volume_cols[
                :, along_depth + 1 : along_depth + 1 + planes, along_rows : along_rows + height, :
            ]
            terms_one.append(
                jnp.einsum("odhw,kdhw->ok", grad_pre, window, preferred_element_type=jnp.float32)
            )
            back_window = rimmed_cols[
                :,
                2 - along_depth : 2 - along_depth + planes,
                2 - along_rows : 2 - along_rows + height,
                :,
            ]
            grad_volume = grad_volume + jnp.einsum(
                "qk,kdhw->qdhw",
                rear_one[along_depth, along_rows],
                back_window,
                preferred_element_type=jnp.float32,
            )
    summed = summed_over(jnp.stack([jnp.stack(terms_one), jnp.stack(terms_two)]), "slab")
    grad_one, grad_two = fold_terms(summed)
    return (output.astype(jnp.bfloat16), grad_volume.astype(jnp.bfloat16), grad_one, grad_two)


def solution(mesh):
    in_specs = (
        P(None, ("grp", "slab"), None, None),
        P(),
        P(),
        P(None, ("grp", "slab"), None, None),
    )
    out_specs = (
        P(None, ("grp", "slab"), None, None),
        P(None, ("grp", "slab"), None, None),
        P("grp", None, None),
        P("grp", None, None),
    )
    return jax.shard_map(
        on_device, mesh=mesh, in_specs=in_specs, out_specs=out_specs, check_vma=False
    )
```

```python
import jax
import numpy as np
import jax.numpy as jnp
from jax import lax
from jax.sharding import PartitionSpec as P


def extended_2(shard, sides, width):
    for axis, dim in sides:
        devices, length = (lax.axis_size(axis), shard.shape[dim])
        up = [(i, (i + 1) % devices) for i in range(devices - 1)]
        down = [(j, i) for i, j in up]
        last = lax.slice_in_dim(shard, length - width, length, axis=dim)
        initial = lax.slice_in_dim(shard, 0, width, axis=dim)
        before = lax.ppermute(last, axis, up)
        after = lax.ppermute(initial, axis, down)
        shard = jnp.concatenate([before, shard, after], axis=dim)
    return shard


def passed_along(block, axis, distance):
    devices = range(lax.axis_size(axis))
    route = [(i - distance, i) for i in devices if i - distance in devices]
    return lax.ppermute(block, axis, route)


def pad_sides(field):
    return jnp.pad(field, ((0, 0), (0, 0), (1, 1), (1, 1)))


def column_stack(field, stride, count, start):
    pieces = []
    for along_cols in range(3):
        first = start(along_cols)
        pieces.append(field[..., first : first + stride * (count - 1) + 1 : stride])
    return jnp.concatenate(pieces, 0)


def summed_over(terms, axis):
    devices = lax.axis_size(axis)
    flat = terms.reshape(-1)
    room = -flat.shape[0] % devices
    flat = jnp.pad(flat, (0, room)).reshape(devices, -1)
    mine = lax.all_to_all(flat, axis, 0, 0, tiled=True).sum(0, keepdims=True)
    whole = lax.all_to_all(jnp.broadcast_to(mine, flat.shape), axis, 0, 0, tiled=True)
    return whole.reshape(-1)[: terms.size].reshape(terms.shape)


def forward_kernel(weights):
    size = weights.shape[1]
    return (
        weights.reshape(3, 3, 3, size, size).transpose(0, 1, 3, 2, 4).reshape(3, 3, size, 3 * size)
    )


def backward_kernel(weights):
    size = weights.shape[1]
    return weights.reshape(3, 3, 3 * size, size)


def fold_term(term):
    size = term.shape[0]
    return term.reshape(size, 3, size).transpose(1, 0, 2)


def fold_terms(summed):
    size = summed.shape[2]
    folded = summed.reshape(2, 9, size, 3, size).transpose(0, 1, 3, 2, 4)
    folded = folded.reshape(2, 27, size, size)
    return folded[0], folded[1]


def gather_terms(listed):
    stacked = jnp.stack(listed)
    return stacked.reshape(27, stacked.shape[2], stacked.shape[3])


def on_device(volume, weight_one, weight_two, cotangent):
    channels, planes, height, columns = volume.shape
    half_planes = planes // 2
    half_rows = height // 2
    half_cols = columns // 2
    front_one = forward_kernel(weight_one)
    front_two = forward_kernel(weight_two)
    rear_one = backward_kernel(weight_one).transpose(0, 1, 3, 2)
    padded = pad_sides(extended_2(volume, (("slab", 1),), 2))
    volume_cols = column_stack(padded, 1, columns, lambda along_cols: along_cols)
    cot_ext = extended_2(cotangent, (("slab", 1),), 1)
    devices = lax.axis_size("slab")
    place = lax.axis_index("slab") * planes + jnp.arange(-1, planes + 1)
    inside = ((place >= 0) & (place < devices * planes))[None, :, None, None]
    preact = jnp.zeros((channels, planes + 2, height, columns), jnp.float32)
    for along_depth in range(3):
        for along_rows in range(3):
            window = volume_cols[
                :, along_depth : along_depth + planes + 2, along_rows : along_rows + height, :
            ]
            preact = preact + jnp.einsum(
                "ok,kdhw->odhw",
                front_one[along_depth, along_rows],
                window,
                preferred_element_type=jnp.float32,
            )
    hidden = jnp.where(inside, jax.nn.silu(preact), 0.0).astype(jnp.bfloat16)
    stacked = hidden[:, : planes + 1]
    stacked = jnp.pad(stacked, ((0, 0), (0, 0), (1, 1), (0, 0)))
    picks = jnp.arange(columns)[:, None, None] == (
        2 * jnp.arange(half_cols)[None, None, :] + jnp.arange(3)[None, :, None] - 1
    )
    hidden_cols = jnp.einsum(
        "qdhp,pck->cqdhk", stacked, picks.astype(jnp.bfloat16), preferred_element_type=jnp.float32
    )
    hidden_cols = hidden_cols.astype(jnp.bfloat16).reshape(
        3 * channels, planes + 1, height + 2, half_cols
    )
    output = jnp.zeros((channels, half_planes, half_rows, half_cols), jnp.float32)
    terms_two = []
    for along_depth in range(3):
        for along_rows in range(3):
            window = hidden_cols[
                :,
                along_depth : along_depth + planes - 1 : 2,
                along_rows : along_rows + height - 1 : 2,
                :,
            ]
            output = output + jnp.einsum(
                "ok,kdhw->odhw",
                front_two[along_depth, along_rows],
                window,
                preferred_element_type=jnp.float32,
            )
            terms_two.append(
                jnp.einsum("odhw,kdhw->ok", cotangent, window, preferred_element_type=jnp.float32)
            )
    rear_two = backward_kernel(weight_two).transpose(0, 1, 3, 2)
    spread = lax.pad(
        cot_ext, jnp.zeros((), cot_ext.dtype), ((0, 0, 0), (0, 1, 1), (1, 2, 1), (1, 2, 1))
    )
    spread_cols = column_stack(spread, 1, columns, lambda along_cols: 2 - along_cols)
    grad_hidden = jnp.zeros((channels, planes + 2, height, columns), jnp.float32)
    for along_depth in range(3):
        for along_rows in range(3):
            back_window = spread_cols[
                :,
                2 - along_depth : 2 - along_depth + planes + 2,
                2 - along_rows : 2 - along_rows + height,
                :,
            ]
            grad_hidden = grad_hidden + jnp.einsum(
                "qk,kdhw->qdhw",
                rear_two[along_depth, along_rows],
                back_window,
                preferred_element_type=jnp.float32,
            )
    sigma = jax.nn.sigmoid(preact)
    grad_rim = grad_hidden * (sigma * (1.0 + preact * (1.0 - sigma)))
    grad_rim = jnp.where(inside, grad_rim, 0.0).astype(jnp.bfloat16)
    grad_pre = grad_rim[:, 1 : planes + 1]
    rimmed = pad_sides(grad_rim)
    rimmed_cols = column_stack(rimmed, 1, columns, lambda along_cols: 2 - along_cols)
    grad_volume = jnp.zeros((channels, planes, height, columns), jnp.float32)
    terms_one = []
    for along_depth in range(3):
        for along_rows in range(3):
            window = volume_cols[
                :, along_depth + 1 : along_depth + 1 + planes, along_rows : along_rows + height, :
            ]
            terms_one.append(
                jnp.einsum("odhw,kdhw->ok", grad_pre, window, preferred_element_type=jnp.float32)
            )
            back_window = rimmed_cols[
                :,
                2 - along_depth : 2 - along_depth + planes,
                2 - along_rows : 2 - along_rows + height,
                :,
            ]
            grad_volume = grad_volume + jnp.einsum(
                "qk,kdhw->qdhw",
                rear_one[along_depth, along_rows],
                back_window,
                preferred_element_type=jnp.float32,
            )
    summed = summed_over(jnp.stack([jnp.stack(terms_one), jnp.stack(terms_two)]), "slab")
    grad_one, grad_two = fold_terms(summed)
    return (output.astype(jnp.bfloat16), grad_volume.astype(jnp.bfloat16), grad_one, grad_two)


def solution(mesh):
    in_specs = (
        P(None, ("grp", "slab"), None, None),
        P(),
        P(),
        P(None, ("grp", "slab"), None, None),
    )
    out_specs = (
        P(None, ("grp", "slab"), None, None),
        P(None, ("grp", "slab"), None, None),
        P("grp", None, None),
        P("grp", None, None),
    )
    return jax.shard_map(
        on_device, mesh=mesh, in_specs=in_specs, out_specs=out_specs, check_vma=False
    )
```

```python
import jax
import numpy as np
import jax.numpy as jnp
from jax import lax
from jax.sharding import PartitionSpec as P


def extended_2(shard, sides, width):
    for axis, dim in sides:
        devices, length = (lax.axis_size(axis), shard.shape[dim])
        up = [(i, (i + 1) % devices) for i in range(devices - 1)]
        down = [(j, i) for i, j in up]
        last = lax.slice_in_dim(shard, length - width, length, axis=dim)
        initial = lax.slice_in_dim(shard, 0, width, axis=dim)
        before = lax.ppermute(last, axis, up)
        after = lax.ppermute(initial, axis, down)
        shard = jnp.concatenate([before, shard, after], axis=dim)
    return shard


def passed_along(block, axis, distance):
    devices = range(lax.axis_size(axis))
    route = [(i - distance, i) for i in devices if i - distance in devices]
    return lax.ppermute(block, axis, route)


def pad_sides(field):
    return jnp.pad(field, ((0, 0), (0, 0), (1, 1), (1, 1)))


def column_stack(field, stride, count, start):
    pieces = []
    for along_cols in range(3):
        first = start(along_cols)
        pieces.append(field[..., first : first + stride * (count - 1) + 1 : stride])
    return jnp.concatenate(pieces, 0)


def summed_over(terms, axis):
    devices = lax.axis_size(axis)
    flat = terms.reshape(-1)
    room = -flat.shape[0] % devices
    flat = jnp.pad(flat, (0, room)).reshape(devices, -1)
    mine = lax.all_to_all(flat, axis, 0, 0, tiled=True).sum(0, keepdims=True)
    whole = lax.all_to_all(jnp.broadcast_to(mine, flat.shape), axis, 0, 0, tiled=True)
    return whole.reshape(-1)[: terms.size].reshape(terms.shape)


def forward_kernel(weights):
    size = weights.shape[1]
    return (
        weights.reshape(3, 3, 3, size, size).transpose(0, 1, 3, 2, 4).reshape(3, 3, size, 3 * size)
    )


def backward_kernel(weights):
    size = weights.shape[1]
    return weights.reshape(3, 3, 3 * size, size)


def fold_term(term):
    size = term.shape[0]
    return term.reshape(size, 3, size).transpose(1, 0, 2)


def fold_terms(summed):
    size = summed.shape[2]
    folded = summed.reshape(2, 9, size, 3, size).transpose(0, 1, 3, 2, 4)
    folded = folded.reshape(2, 27, size, size)
    return folded[0], folded[1]


def gather_terms(listed):
    stacked = jnp.stack(listed)
    return stacked.reshape(27, stacked.shape[2], stacked.shape[3])


def on_device(volume, weight_one, weight_two, cotangent):
    channels, planes, height, columns = volume.shape
    half_planes = planes // 2
    half_rows = height // 2
    half_cols = columns // 2
    front_one = forward_kernel(weight_one)
    front_two = forward_kernel(weight_two)
    rear_one = backward_kernel(weight_one).transpose(0, 1, 3, 2)
    padded = pad_sides(extended_2(volume, (("slab", 1),), 2))
    volume_cols = column_stack(padded, 1, columns, lambda along_cols: along_cols)
    cot_ext = extended_2(cotangent, (("slab", 1),), 1)
    devices = lax.axis_size("slab")
    place = lax.axis_index("slab") * planes + jnp.arange(-1, planes + 1)
    inside = ((place >= 0) & (place < devices * planes))[None, :, None, None]
    preact = jnp.zeros((channels, planes + 2, height, columns), jnp.float32)
    for along_depth in range(3):
        for along_rows in range(3):
            window = volume_cols[
                :, along_depth : along_depth + planes + 2, along_rows : along_rows + height, :
            ]
            preact = preact + jnp.einsum(
                "ok,kdhw->odhw",
                front_one[along_depth, along_rows],
                window,
                preferred_element_type=jnp.float32,
            )
    hidden = jnp.where(inside, jax.nn.silu(preact), 0.0).astype(jnp.bfloat16)
    stacked = hidden[:, : planes + 1]
    stacked = jnp.pad(stacked, ((0, 0), (0, 0), (1, 1), (0, 0)))
    picks = jnp.arange(columns)[:, None, None] == (
        2 * jnp.arange(half_cols)[None, None, :] + jnp.arange(3)[None, :, None] - 1
    )
    hidden_cols = jnp.einsum(
        "qdhp,pck->cqdhk", stacked, picks.astype(jnp.bfloat16), preferred_element_type=jnp.float32
    )
    hidden_cols = hidden_cols.astype(jnp.bfloat16).reshape(
        3 * channels, planes + 1, height + 2, half_cols
    )
    output = jnp.zeros((channels, half_planes, half_rows, half_cols), jnp.float32)
    terms_two = []
    for along_depth in range(3):
        for along_rows in range(3):
            window = hidden_cols[
                :,
                along_depth : along_depth + planes - 1 : 2,
                along_rows : along_rows + height - 1 : 2,
                :,
            ]
            output = output + jnp.einsum(
                "ok,kdhw->odhw",
                front_two[along_depth, along_rows],
                window,
                preferred_element_type=jnp.float32,
            )
            terms_two.append(
                jnp.einsum("odhw,kdhw->ok", cotangent, window, preferred_element_type=jnp.float32)
            )
    extended = jnp.pad(cot_ext, ((0, 0), (0, 1), (0, 1), (0, 1)))
    class_planes = half_planes + 1
    parity_taps = [[(1, 0)], [(2, 0), (0, 1)]]
    depth_taps = [[(2, 0), (0, 1)], [(1, 1)]]
    order = []
    for depth_parity in range(2):
        for row_parity in range(2):
            for col_parity in range(2):
                for tap_depth, _ in depth_taps[depth_parity]:
                    for tap_row, _ in parity_taps[row_parity]:
                        for tap_col, _ in parity_taps[col_parity]:
                            order.append(9 * tap_depth + 3 * tap_row + tap_col)
    ordered_two = weight_two[np.array(order)]
    taken = 0
    classes = []
    for depth_parity in range(2):
        for row_parity in range(2):
            for col_parity in range(2):
                pieces = []
                for tap_depth, skip_depth in depth_taps[depth_parity]:
                    for tap_row, skip_row in parity_taps[row_parity]:
                        for tap_col, skip_col in parity_taps[col_parity]:
                            pieces.append(
                                extended[
                                    :,
                                    skip_depth : skip_depth + class_planes,
                                    skip_row : skip_row + half_rows,
                                    skip_col : skip_col + half_cols,
                                ]
                            )
                joined = jnp.concatenate(pieces, 0)
                joined_kernel = ordered_two[taken : taken + len(pieces)].reshape(-1, channels)
                taken += len(pieces)
                classes.append(
                    jnp.einsum(
                        "kq,kdhw->qdhw", joined_kernel, joined, preferred_element_type=jnp.float32
                    )
                )
    parity_grid = jnp.stack(classes).reshape(2, 2, 2, channels, class_planes, half_rows, half_cols)
    grad_hidden = parity_grid.transpose(3, 4, 0, 5, 1, 6, 2).reshape(
        channels, 2 * class_planes, height, columns
    )
    sigma = jax.nn.sigmoid(preact)
    grad_rim = grad_hidden * (sigma * (1.0 + preact * (1.0 - sigma)))
    grad_rim = jnp.where(inside, grad_rim, 0.0).astype(jnp.bfloat16)
    grad_pre = grad_rim[:, 1 : planes + 1]
    rimmed = pad_sides(grad_rim)
    rimmed_cols = column_stack(rimmed, 1, columns, lambda along_cols: 2 - along_cols)
    grad_volume = jnp.zeros((channels, planes, height, columns), jnp.float32)
    terms_one = []
    for along_depth in range(3):
        for along_rows in range(3):
            window = volume_cols[
                :, along_depth + 1 : along_depth + 1 + planes, along_rows : along_rows + height, :
            ]
            terms_one.append(
                jnp.einsum("odhw,kdhw->ok", grad_pre, window, preferred_element_type=jnp.float32)
            )
            back_window = rimmed_cols[
                :,
                2 - along_depth : 2 - along_depth + planes,
                2 - along_rows : 2 - along_rows + height,
                :,
            ]
            grad_volume = grad_volume + jnp.einsum(
                "qk,kdhw->qdhw",
                rear_one[along_depth, along_rows],
                back_window,
                preferred_element_type=jnp.float32,
            )
    summed = summed_over(jnp.stack([jnp.stack(terms_one), jnp.stack(terms_two)]), "slab")
    grad_one, grad_two = fold_terms(summed)
    return (output.astype(jnp.bfloat16), grad_volume.astype(jnp.bfloat16), grad_one, grad_two)


def solution(mesh):
    in_specs = (
        P(None, ("grp", "slab"), None, None),
        P(),
        P(),
        P(None, ("grp", "slab"), None, None),
    )
    out_specs = (
        P(None, ("grp", "slab"), None, None),
        P(None, ("grp", "slab"), None, None),
        P("grp", None, None),
        P("grp", None, None),
    )
    return jax.shard_map(
        on_device, mesh=mesh, in_specs=in_specs, out_specs=out_specs, check_vma=False
    )
```

```python
import jax
import numpy as np
import jax.numpy as jnp
from jax import lax
from jax.sharding import PartitionSpec as P


def extended_2(shard, sides, width):
    for axis, dim in sides:
        devices, length = (lax.axis_size(axis), shard.shape[dim])
        up = [(i, (i + 1) % devices) for i in range(devices - 1)]
        down = [(j, i) for i, j in up]
        last = lax.slice_in_dim(shard, length - width, length, axis=dim)
        initial = lax.slice_in_dim(shard, 0, width, axis=dim)
        before = lax.ppermute(last, axis, up)
        after = lax.ppermute(initial, axis, down)
        shard = jnp.concatenate([before, shard, after], axis=dim)
    return shard


def passed_along(block, axis, distance):
    devices = range(lax.axis_size(axis))
    route = [(i - distance, i) for i in devices if i - distance in devices]
    return lax.ppermute(block, axis, route)


def pad_sides(field):
    return jnp.pad(field, ((0, 0), (0, 0), (1, 1), (1, 1)))


def column_stack(field, stride, count, start):
    pieces = []
    for along_cols in range(3):
        first = start(along_cols)
        pieces.append(field[..., first : first + stride * (count - 1) + 1 : stride])
    return jnp.concatenate(pieces, 0)


def summed_over(terms, axis):
    devices = lax.axis_size(axis)
    flat = terms.reshape(-1)
    room = -flat.shape[0] % devices
    flat = jnp.pad(flat, (0, room)).reshape(devices, -1)
    mine = lax.all_to_all(flat, axis, 0, 0, tiled=True).sum(0, keepdims=True)
    whole = lax.all_to_all(jnp.broadcast_to(mine, flat.shape), axis, 0, 0, tiled=True)
    return whole.reshape(-1)[: terms.size].reshape(terms.shape)


def forward_kernel(weights):
    size = weights.shape[1]
    return (
        weights.reshape(3, 3, 3, size, size).transpose(0, 1, 3, 2, 4).reshape(3, 3, size, 3 * size)
    )


def backward_kernel(weights):
    size = weights.shape[1]
    return weights.reshape(3, 3, 3 * size, size)


def fold_term(term):
    size = term.shape[0]
    return term.reshape(size, 3, size).transpose(1, 0, 2)


def fold_terms(summed):
    size = summed.shape[2]
    folded = summed.reshape(2, 9, size, 3, size).transpose(0, 1, 3, 2, 4)
    folded = folded.reshape(2, 27, size, size)
    return folded[0], folded[1]


def gather_terms(listed):
    stacked = jnp.stack(listed)
    return stacked.reshape(27, stacked.shape[2], stacked.shape[3])


def on_device(volume, weight_one, weight_two, cotangent):
    channels, planes, height, columns = volume.shape
    half_planes = planes // 2
    half_rows = height // 2
    half_cols = columns // 2
    front_one = forward_kernel(weight_one)
    front_two = forward_kernel(weight_two)
    rear_one = backward_kernel(weight_one).transpose(0, 1, 3, 2)
    padded = pad_sides(extended_2(volume, (("slab", 1),), 2))
    volume_cols = column_stack(padded, 1, columns, lambda along_cols: along_cols)
    cot_ext = extended_2(cotangent, (("slab", 1),), 1)
    devices = lax.axis_size("slab")
    place = lax.axis_index("slab") * planes + jnp.arange(-1, planes + 1)
    inside = ((place >= 0) & (place < devices * planes))[None, :, None, None]
    preact = jnp.zeros((channels, planes + 2, height, columns), jnp.float32)
    for along_depth in range(3):
        for along_rows in range(3):
            window = volume_cols[
                :, along_depth : along_depth + planes + 2, along_rows : along_rows + height, :
            ]
            preact = preact + jnp.einsum(
                "ok,kdhw->odhw",
                front_one[along_depth, along_rows],
                window,
                preferred_element_type=jnp.float32,
            )
    hidden = jnp.where(inside, jax.nn.silu(preact), 0.0).astype(jnp.bfloat16)
    stacked = hidden[:, : planes + 1]
    stacked = jnp.pad(stacked, ((0, 0), (0, 0), (1, 1), (0, 0)))
    picks = jnp.arange(columns)[:, None, None] == (
        2 * jnp.arange(half_cols)[None, None, :] + jnp.arange(3)[None, :, None] - 1
    )
    hidden_cols = jnp.einsum(
        "qdhp,pck->cqdhk", stacked, picks.astype(jnp.bfloat16), preferred_element_type=jnp.float32
    )
    hidden_cols = hidden_cols.astype(jnp.bfloat16).reshape(
        3 * channels, planes + 1, height + 2, half_cols
    )
    output = jnp.zeros((channels, half_planes, half_rows, half_cols), jnp.float32)
    terms_two = []
    for along_depth in range(3):
        for along_rows in range(3):
            window = hidden_cols[
                :,
                along_depth : along_depth + planes - 1 : 2,
                along_rows : along_rows + height - 1 : 2,
                :,
            ]
            output = output + jnp.einsum(
                "ok,kdhw->odhw",
                front_two[along_depth, along_rows],
                window,
                preferred_element_type=jnp.float32,
            )
            terms_two.append(
                jnp.einsum("odhw,kdhw->ok", cotangent, window, preferred_element_type=jnp.float32)
            )
    extended = jnp.pad(cot_ext, ((0, 0), (0, 1), (0, 1), (0, 1)))
    class_planes = half_planes + 1
    parity_taps = [[(1, 0)], [(2, 0), (0, 1)]]
    depth_taps = [[(2, 0), (0, 1)], [(1, 1)]]
    order = []
    for depth_parity in range(2):
        for row_parity in range(2):
            for col_parity in range(2):
                for tap_depth, _ in depth_taps[depth_parity]:
                    for tap_row, _ in parity_taps[row_parity]:
                        for tap_col, _ in parity_taps[col_parity]:
                            order.append(9 * tap_depth + 3 * tap_row + tap_col)
    ordered_two = weight_two[np.array(order)]
    taken = 0
    classes = []
    for depth_parity in range(2):
        for row_parity in range(2):
            for col_parity in range(2):
                pieces = []
                for tap_depth, skip_depth in depth_taps[depth_parity]:
                    for tap_row, skip_row in parity_taps[row_parity]:
                        for tap_col, skip_col in parity_taps[col_parity]:
                            pieces.append(
                                extended[
                                    :,
                                    skip_depth : skip_depth + class_planes,
                                    skip_row : skip_row + half_rows,
                                    skip_col : skip_col + half_cols,
                                ]
                            )
                joined = jnp.concatenate(pieces, 0)
                joined_kernel = ordered_two[taken : taken + len(pieces)].reshape(-1, channels)
                taken += len(pieces)
                classes.append(
                    jnp.einsum(
                        "kq,kdhw->qdhw", joined_kernel, joined, preferred_element_type=jnp.float32
                    )
                )
    parity_grid = jnp.stack(classes).astype(jnp.bfloat16).reshape(2, 2, 2, channels, class_planes, half_rows, half_cols)
    grad_hidden = parity_grid.transpose(3, 4, 0, 5, 1, 6, 2).reshape(
        channels, 2 * class_planes, height, columns
    )
    sigma = jax.nn.sigmoid(preact)
    grad_rim = grad_hidden.astype(jnp.float32) * (sigma * (1.0 + preact * (1.0 - sigma)))
    grad_rim = jnp.where(inside, grad_rim, 0.0).astype(jnp.bfloat16)
    grad_pre = grad_rim[:, 1 : planes + 1]
    rimmed = pad_sides(grad_rim)
    rimmed_cols = column_stack(rimmed, 1, columns, lambda along_cols: 2 - along_cols)
    grad_volume = jnp.zeros((channels, planes, height, columns), jnp.float32)
    terms_one = []
    for along_depth in range(3):
        for along_rows in range(3):
            window = volume_cols[
                :, along_depth + 1 : along_depth + 1 + planes, along_rows : along_rows + height, :
            ]
            terms_one.append(
                jnp.einsum("odhw,kdhw->ok", grad_pre, window, preferred_element_type=jnp.float32)
            )
            back_window = rimmed_cols[
                :,
                2 - along_depth : 2 - along_depth + planes,
                2 - along_rows : 2 - along_rows + height,
                :,
            ]
            grad_volume = grad_volume + jnp.einsum(
                "qk,kdhw->qdhw",
                rear_one[along_depth, along_rows],
                back_window,
                preferred_element_type=jnp.float32,
            )
    summed = summed_over(jnp.stack([jnp.stack(terms_one), jnp.stack(terms_two)]), "slab")
    grad_one, grad_two = fold_terms(summed)
    return (output.astype(jnp.bfloat16), grad_volume.astype(jnp.bfloat16), grad_one, grad_two)


def solution(mesh):
    in_specs = (
        P(None, ("grp", "slab"), None, None),
        P(),
        P(),
        P(None, ("grp", "slab"), None, None),
    )
    out_specs = (
        P(None, ("grp", "slab"), None, None),
        P(None, ("grp", "slab"), None, None),
        P("grp", None, None),
        P("grp", None, None),
    )
    return jax.shard_map(
        on_device, mesh=mesh, in_specs=in_specs, out_specs=out_specs, check_vma=False
    )
```

```python
import jax
import numpy as np
import jax.numpy as jnp
from jax import lax
from jax.sharding import PartitionSpec as P


def extended_2(shard, sides, width):
    for axis, dim in sides:
        devices, length = (lax.axis_size(axis), shard.shape[dim])
        up = [(i, (i + 1) % devices) for i in range(devices - 1)]
        down = [(j, i) for i, j in up]
        last = lax.slice_in_dim(shard, length - width, length, axis=dim)
        initial = lax.slice_in_dim(shard, 0, width, axis=dim)
        before = lax.ppermute(last, axis, up)
        after = lax.ppermute(initial, axis, down)
        shard = jnp.concatenate([before, shard, after], axis=dim)
    return shard


def passed_along(block, axis, distance):
    devices = range(lax.axis_size(axis))
    route = [(i - distance, i) for i in devices if i - distance in devices]
    return lax.ppermute(block, axis, route)


def pad_sides(field):
    return jnp.pad(field, ((0, 0), (0, 0), (1, 1), (1, 1)))


def column_stack(field, stride, count, start):
    pieces = []
    for along_cols in range(3):
        first = start(along_cols)
        pieces.append(field[..., first : first + stride * (count - 1) + 1 : stride])
    return jnp.concatenate(pieces, 0)


def summed_over(terms, axis):
    devices = lax.axis_size(axis)
    flat = terms.reshape(-1)
    room = -flat.shape[0] % devices
    flat = jnp.pad(flat, (0, room)).reshape(devices, -1)
    mine = lax.all_to_all(flat, axis, 0, 0, tiled=True).sum(0, keepdims=True)
    whole = lax.all_to_all(jnp.broadcast_to(mine, flat.shape), axis, 0, 0, tiled=True)
    return whole.reshape(-1)[: terms.size].reshape(terms.shape)


def forward_kernel(weights):
    size = weights.shape[1]
    return (
        weights.reshape(3, 3, 3, size, size).transpose(0, 1, 3, 2, 4).reshape(3, 3, size, 3 * size)
    )


def backward_kernel(weights):
    size = weights.shape[1]
    return weights.reshape(3, 3, 3 * size, size)


def fold_term(term):
    size = term.shape[0]
    return term.reshape(size, 3, size).transpose(1, 0, 2)


def fold_terms(summed):
    size = summed.shape[2]
    folded = summed.reshape(2, 9, size, 3, size).transpose(0, 1, 3, 2, 4)
    folded = folded.reshape(2, 27, size, size)
    return folded[0], folded[1]


def gather_terms(listed):
    stacked = jnp.stack(listed)
    return stacked.reshape(27, stacked.shape[2], stacked.shape[3])


def on_device(volume, weight_one, weight_two, cotangent):
    channels, planes, height, columns = volume.shape
    half_planes = planes // 2
    half_rows = height // 2
    half_cols = columns // 2
    front_one = forward_kernel(weight_one)
    front_two = forward_kernel(weight_two)
    rear_one = backward_kernel(weight_one).transpose(0, 1, 3, 2)
    padded = pad_sides(extended_2(volume, (("slab", 1),), 2))
    volume_cols = column_stack(padded, 1, columns, lambda along_cols: along_cols)
    cot_ext = extended_2(cotangent, (("slab", 1),), 1)
    devices = lax.axis_size("slab")
    place = lax.axis_index("slab") * planes + jnp.arange(-1, planes + 1)
    inside = ((place >= 0) & (place < devices * planes))[None, :, None, None]
    preact = jnp.zeros((channels, planes + 2, height, columns), jnp.float32)
    for along_depth in range(3):
        for along_rows in range(3):
            window = volume_cols[
                :, along_depth : along_depth + planes + 2, along_rows : along_rows + height, :
            ]
            preact = preact + jnp.einsum(
                "ok,kdhw->odhw",
                front_one[along_depth, along_rows],
                window,
                preferred_element_type=jnp.float32,
            )
    hidden = jnp.where(inside, jax.nn.silu(preact), 0.0).astype(jnp.bfloat16)
    stacked = hidden[:, : planes + 1]
    stacked = jnp.pad(stacked, ((0, 0), (0, 0), (1, 1), (0, 0)))
    picks = jnp.arange(columns)[:, None, None] == (
        2 * jnp.arange(half_cols)[None, None, :] + jnp.arange(3)[None, :, None] - 1
    )
    hidden_cols = jnp.einsum(
        "qdhp,pck->cqdhk", stacked, picks.astype(jnp.bfloat16), preferred_element_type=jnp.float32
    )
    hidden_cols = hidden_cols.astype(jnp.bfloat16).reshape(
        3 * channels, planes + 1, height + 2, half_cols
    )
    output = jnp.zeros((channels, half_planes, half_rows, half_cols), jnp.float32)
    terms_two = []
    for along_depth in range(3):
        for along_rows in range(3):
            window = hidden_cols[
                :,
                along_depth : along_depth + planes - 1 : 2,
                along_rows : along_rows + height - 1 : 2,
                :,
            ]
            output = output + jnp.einsum(
                "ok,kdhw->odhw",
                front_two[along_depth, along_rows],
                window,
                preferred_element_type=jnp.float32,
            )
            terms_two.append(
                jnp.einsum("odhw,kdhw->ok", cotangent, window, preferred_element_type=jnp.float32)
            )
    extended = jnp.pad(cot_ext, ((0, 0), (0, 0), (0, 1), (0, 0)))
    spread = jnp.arange(half_cols)[:, None, None] * 2 + jnp.arange(3)[None, :, None] - 1
    spread = (spread == jnp.arange(columns)[None, None, :]).astype(jnp.bfloat16)
    widened = jnp.einsum("odrj,jcw->codrw", extended, spread, preferred_element_type=jnp.float32)
    widened = widened.astype(jnp.bfloat16)
    class_planes = half_planes + 1
    row_taps = [[(1, 0)], [(2, 0), (0, 1)]]
    depth_taps = [[(2, 0), (0, 1)], [(1, 1)]]
    order = []
    for depth_slot in range(2):
        for row_parity in range(2):
            for tap_depth, _ in depth_taps[depth_slot]:
                for tap_row, _ in row_taps[row_parity]:
                    for tap_col in range(3):
                        order.append(9 * tap_depth + 3 * tap_row + tap_col)
    ordered_two = weight_two[np.array(order)]
    taken = 0
    classes = []
    for depth_slot in range(2):
        for row_parity in range(2):
            pieces = []
            for tap_depth, skip_depth in depth_taps[depth_slot]:
                for tap_row, skip_row in row_taps[row_parity]:
                    for tap_col in range(3):
                        pieces.append(
                            widened[
                                tap_col,
                                :,
                                skip_depth : skip_depth + class_planes,
                                skip_row : skip_row + half_rows,
                                :,
                            ]
                        )
            joined = jnp.concatenate(pieces, 0)
            joined_kernel = ordered_two[taken : taken + len(pieces)].reshape(-1, channels)
            taken += len(pieces)
            classes.append(
                jnp.einsum("kq,kdhw->qdhw", joined_kernel, joined, preferred_element_type=jnp.float32)
            )
    parity_grid = jnp.stack(classes).reshape(2, 2, channels, class_planes, half_rows, columns)
    grad_hidden = parity_grid.transpose(2, 3, 0, 4, 1, 5).reshape(
        channels, 2 * class_planes, height, columns
    )
    sigma = jax.nn.sigmoid(preact)
    grad_rim = grad_hidden * (sigma * (1.0 + preact * (1.0 - sigma)))
    grad_rim = jnp.where(inside, grad_rim, 0.0).astype(jnp.bfloat16)
    grad_pre = grad_rim[:, 1 : planes + 1]
    rimmed = pad_sides(grad_rim)
    rimmed_cols = column_stack(rimmed, 1, columns, lambda along_cols: 2 - along_cols)
    grad_volume = jnp.zeros((channels, planes, height, columns), jnp.float32)
    terms_one = []
    for along_depth in range(3):
        for along_rows in range(3):
            window = volume_cols[
                :, along_depth + 1 : along_depth + 1 + planes, along_rows : along_rows + height, :
            ]
            terms_one.append(
                jnp.einsum("odhw,kdhw->ok", grad_pre, window, preferred_element_type=jnp.float32)
            )
            back_window = rimmed_cols[
                :,
                2 - along_depth : 2 - along_depth + planes,
                2 - along_rows : 2 - along_rows + height,
                :,
            ]
            grad_volume = grad_volume + jnp.einsum(
                "qk,kdhw->qdhw",
                rear_one[along_depth, along_rows],
                back_window,
                preferred_element_type=jnp.float32,
            )
    summed = summed_over(jnp.stack([jnp.stack(terms_one), jnp.stack(terms_two)]), "slab")
    grad_one, grad_two = fold_terms(summed)
    return (output.astype(jnp.bfloat16), grad_volume.astype(jnp.bfloat16), grad_one, grad_two)


def solution(mesh):
    in_specs = (
        P(None, ("grp", "slab"), None, None),
        P(),
        P(),
        P(None, ("grp", "slab"), None, None),
    )
    out_specs = (
        P(None, ("grp", "slab"), None, None),
        P(None, ("grp", "slab"), None, None),
        P("grp", None, None),
        P("grp", None, None),
    )
    return jax.shard_map(
        on_device, mesh=mesh, in_specs=in_specs, out_specs=out_specs, check_vma=False
    )
```

```python
import jax
import numpy as np
import jax.numpy as jnp
from jax import lax
from jax.sharding import PartitionSpec as P


def extended_2(shard, sides, width):
    for axis, dim in sides:
        devices, length = (lax.axis_size(axis), shard.shape[dim])
        up = [(i, (i + 1) % devices) for i in range(devices - 1)]
        down = [(j, i) for i, j in up]
        last = lax.slice_in_dim(shard, length - width, length, axis=dim)
        initial = lax.slice_in_dim(shard, 0, width, axis=dim)
        before = lax.ppermute(last, axis, up)
        after = lax.ppermute(initial, axis, down)
        shard = jnp.concatenate([before, shard, after], axis=dim)
    return shard


def passed_along(block, axis, distance):
    devices = range(lax.axis_size(axis))
    route = [(i - distance, i) for i in devices if i - distance in devices]
    return lax.ppermute(block, axis, route)


def pad_sides(field):
    return jnp.pad(field, ((0, 0), (0, 0), (1, 1), (1, 1)))


def column_stack(field, stride, count, start):
    pieces = []
    for along_cols in range(3):
        first = start(along_cols)
        pieces.append(field[..., first : first + stride * (count - 1) + 1 : stride])
    return jnp.concatenate(pieces, 0)


def summed_over(terms, axis):
    devices = lax.axis_size(axis)
    flat = terms.reshape(-1)
    room = -flat.shape[0] % devices
    flat = jnp.pad(flat, (0, room)).reshape(devices, -1)
    mine = lax.all_to_all(flat, axis, 0, 0, tiled=True).sum(0, keepdims=True)
    whole = lax.all_to_all(jnp.broadcast_to(mine, flat.shape), axis, 0, 0, tiled=True)
    return whole.reshape(-1)[: terms.size].reshape(terms.shape)


def forward_kernel(weights):
    size = weights.shape[1]
    return (
        weights.reshape(3, 3, 3, size, size).transpose(0, 1, 3, 2, 4).reshape(3, 3, size, 3 * size)
    )


def backward_kernel(weights):
    size = weights.shape[1]
    return weights.reshape(3, 3, 3 * size, size)


def fold_term(term):
    size = term.shape[0]
    return term.reshape(size, 3, size).transpose(1, 0, 2)


def fold_terms(summed):
    size = summed.shape[2]
    folded = summed.reshape(2, 9, size, 3, size).transpose(0, 1, 3, 2, 4)
    folded = folded.reshape(2, 27, size, size)
    return folded[0], folded[1]


def gather_terms(listed):
    stacked = jnp.stack(listed)
    return stacked.reshape(27, stacked.shape[2], stacked.shape[3])


def on_device(volume, weight_one, weight_two, cotangent):
    channels, planes, height, columns = volume.shape
    half_planes = planes // 2
    half_rows = height // 2
    half_cols = columns // 2
    front_one = forward_kernel(weight_one)
    front_two = forward_kernel(weight_two)
    rear_one = backward_kernel(weight_one).transpose(0, 1, 3, 2)
    padded = pad_sides(extended_2(volume, (("slab", 1),), 2))
    volume_cols = column_stack(padded, 1, columns, lambda along_cols: along_cols)
    cot_ext = extended_2(cotangent, (("slab", 1),), 1)
    devices = lax.axis_size("slab")
    place = lax.axis_index("slab") * planes + jnp.arange(-1, planes + 1)
    inside = ((place >= 0) & (place < devices * planes))[None, :, None, None]
    preact = jnp.zeros((channels, planes + 2, height, columns), jnp.float32)
    for along_depth in range(3):
        for along_rows in range(3):
            window = volume_cols[
                :, along_depth : along_depth + planes + 2, along_rows : along_rows + height, :
            ]
            preact = preact + jnp.einsum(
                "ok,kdhw->odhw",
                front_one[along_depth, along_rows],
                window,
                preferred_element_type=jnp.float32,
            )
    hidden = jnp.where(inside, jax.nn.silu(preact), 0.0).astype(jnp.bfloat16)
    stacked = hidden[:, : planes + 1]
    stacked = jnp.pad(stacked, ((0, 0), (0, 0), (1, 1), (0, 0)))
    picks = jnp.arange(columns)[:, None, None] == (
        2 * jnp.arange(half_cols)[None, None, :] + jnp.arange(3)[None, :, None] - 1
    )
    hidden_cols = jnp.einsum(
        "qdhp,pck->cqdhk", stacked, picks.astype(jnp.bfloat16), preferred_element_type=jnp.float32
    )
    hidden_cols = hidden_cols.astype(jnp.bfloat16).reshape(
        3 * channels, planes + 1, height + 2, half_cols
    )
    output = jnp.zeros((channels, half_planes, half_rows, half_cols), jnp.float32)
    terms_two = []
    for along_depth in range(3):
        for along_rows in range(3):
            window = hidden_cols[
                :,
                along_depth : along_depth + planes - 1 : 2,
                along_rows : along_rows + height - 1 : 2,
                :,
            ]
            output = output + jnp.einsum(
                "ok,kdhw->odhw",
                front_two[along_depth, along_rows],
                window,
                preferred_element_type=jnp.float32,
            )
            terms_two.append(
                jnp.einsum("odhw,kdhw->ok", cotangent, window, preferred_element_type=jnp.float32)
            )
    extended = jnp.pad(cot_ext, ((0, 0), (0, 0), (0, 1), (0, 0)))
    spread = jnp.arange(half_cols)[:, None, None] * 2 + jnp.arange(3)[None, :, None] - 1
    spread = (spread == jnp.arange(columns)[None, None, :]).astype(jnp.bfloat16)
    widened = jnp.einsum("odrj,jcw->codrw", extended, spread, preferred_element_type=jnp.float32)
    widened = widened.astype(jnp.bfloat16)
    class_planes = half_planes + 1
    row_taps = [[(1, 0)], [(2, 0), (0, 1)]]
    depth_taps = [[(2, 0), (0, 1)], [(1, 1)]]
    order = []
    for depth_slot in range(2):
        for row_parity in range(2):
            for tap_depth, _ in depth_taps[depth_slot]:
                for tap_row, _ in row_taps[row_parity]:
                    for tap_col in range(3):
                        order.append(9 * tap_depth + 3 * tap_row + tap_col)
    ordered_two = weight_two[np.array(order)]
    taken = 0
    classes = []
    for depth_slot in range(2):
        for row_parity in range(2):
            pieces = []
            for tap_depth, skip_depth in depth_taps[depth_slot]:
                for tap_row, skip_row in row_taps[row_parity]:
                    for tap_col in range(3):
                        pieces.append(
                            widened[
                                tap_col,
                                :,
                                skip_depth : skip_depth + class_planes,
                                skip_row : skip_row + half_rows,
                                :,
                            ]
                        )
            joined = jnp.concatenate(pieces, 0)
            joined_kernel = ordered_two[taken : taken + len(pieces)].reshape(-1, channels)
            taken += len(pieces)
            classes.append(
                jnp.einsum("kq,kdhw->qdhw", joined_kernel, joined, preferred_element_type=jnp.float32)
            )
    parity_grid = jnp.stack(classes).reshape(2, 2, channels, class_planes, half_rows, columns)
    grad_hidden = parity_grid.transpose(2, 3, 0, 4, 1, 5).reshape(
        channels, 2 * class_planes, height, columns
    )
    sigma = jax.nn.sigmoid(preact)
    grad_rim = grad_hidden * (sigma * (1.0 + preact * (1.0 - sigma)))
    grad_rim = jnp.where(inside, grad_rim, 0.0).astype(jnp.bfloat16)
    grad_pre = grad_rim[:, 1 : planes + 1]
    rimmed = pad_sides(grad_rim)
    rimmed_cols = column_stack(rimmed, 1, columns, lambda along_cols: 2 - along_cols)
    grad_volume = jnp.zeros((channels, planes, height, columns), jnp.float32)
    terms_one = []
    for along_depth in range(3):
        for along_rows in range(3):
            window = volume_cols[
                :, along_depth + 1 : along_depth + 1 + planes, along_rows : along_rows + height, :
            ]
            terms_one.append(
                jnp.einsum("odhw,kdhw->ok", grad_pre, window, preferred_element_type=jnp.float32)
            )
            back_window = rimmed_cols[
                :,
                2 - along_depth : 2 - along_depth + planes,
                2 - along_rows : 2 - along_rows + height,
                :,
            ]
            grad_volume = grad_volume + jnp.einsum(
                "qk,kdhw->qdhw",
                rear_one[along_depth, along_rows],
                back_window,
                preferred_element_type=jnp.float32,
            )
    folded = fold_terms(jnp.stack([jnp.stack(terms_one), jnp.stack(terms_two)]))
    grad_one, grad_two = summed_over(jnp.stack(folded), "slab")
    return (output.astype(jnp.bfloat16), grad_volume.astype(jnp.bfloat16), grad_one, grad_two)


def solution(mesh):
    in_specs = (
        P(None, ("grp", "slab"), None, None),
        P(),
        P(),
        P(None, ("grp", "slab"), None, None),
    )
    out_specs = (
        P(None, ("grp", "slab"), None, None),
        P(None, ("grp", "slab"), None, None),
        P("grp", None, None),
        P("grp", None, None),
    )
    return jax.shard_map(
        on_device, mesh=mesh, in_specs=in_specs, out_specs=out_specs, check_vma=False
    )
```

```python
import jax
import numpy as np
import jax.numpy as jnp
from jax import lax
from jax.sharding import PartitionSpec as P


def extended_2(shard, sides, width):
    for axis, dim in sides:
        devices, length = (lax.axis_size(axis), shard.shape[dim])
        up = [(i, (i + 1) % devices) for i in range(devices - 1)]
        down = [(j, i) for i, j in up]
        last = lax.slice_in_dim(shard, length - width, length, axis=dim)
        initial = lax.slice_in_dim(shard, 0, width, axis=dim)
        before = lax.ppermute(last, axis, up)
        after = lax.ppermute(initial, axis, down)
        shard = jnp.concatenate([before, shard, after], axis=dim)
    return shard


def passed_along(block, axis, distance):
    devices = range(lax.axis_size(axis))
    route = [(i - distance, i) for i in devices if i - distance in devices]
    return lax.ppermute(block, axis, route)


def pad_sides(field):
    return jnp.pad(field, ((0, 0), (0, 0), (1, 1), (1, 1)))


def column_stack(field, stride, count, start):
    pieces = []
    for along_cols in range(3):
        first = start(along_cols)
        pieces.append(field[..., first : first + stride * (count - 1) + 1 : stride])
    return jnp.concatenate(pieces, 0)


def summed_over(terms, axis):
    devices = lax.axis_size(axis)
    flat = terms.reshape(-1)
    room = -flat.shape[0] % devices
    flat = jnp.pad(flat, (0, room)).reshape(devices, -1)
    mine = lax.all_to_all(flat, axis, 0, 0, tiled=True).sum(0, keepdims=True)
    whole = lax.all_to_all(jnp.broadcast_to(mine, flat.shape), axis, 0, 0, tiled=True)
    return whole.reshape(-1)[: terms.size].reshape(terms.shape)


def forward_kernel(weights):
    size = weights.shape[1]
    return (
        weights.reshape(3, 3, 3, size, size).transpose(0, 1, 3, 2, 4).reshape(3, 3, size, 3 * size)
    )


def backward_kernel(weights):
    size = weights.shape[1]
    return weights.reshape(3, 3, 3 * size, size)


def fold_term(term):
    size = term.shape[0]
    return term.reshape(size, 3, size).transpose(1, 0, 2)


def fold_terms(summed):
    size = summed.shape[2]
    folded = summed.reshape(2, 9, size, 3, size).transpose(0, 1, 3, 2, 4)
    folded = folded.reshape(2, 27, size, size)
    return folded[0], folded[1]


def gather_terms(listed):
    stacked = jnp.stack(listed)
    return stacked.reshape(27, stacked.shape[2], stacked.shape[3])


def on_device(volume, weight_one, weight_two, cotangent):
    channels, planes, height, columns = volume.shape
    half_planes = planes // 2
    half_rows = height // 2
    half_cols = columns // 2
    front_one = forward_kernel(weight_one)
    front_two = forward_kernel(weight_two)
    rear_one = backward_kernel(weight_one).transpose(0, 1, 3, 2)
    padded = pad_sides(extended_2(volume, (("slab", 1),), 2))
    volume_cols = column_stack(padded, 1, columns, lambda along_cols: along_cols)
    cot_ext = extended_2(cotangent, (("slab", 1),), 1)
    devices = lax.axis_size("slab")
    place = lax.axis_index("slab") * planes + jnp.arange(-1, planes + 1)
    inside = ((place >= 0) & (place < devices * planes))[None, :, None, None]
    preact = jnp.zeros((channels, planes + 2, height, columns), jnp.float32)
    for along_depth in range(3):
        for along_rows in range(3):
            window = volume_cols[
                :, along_depth : along_depth + planes + 2, along_rows : along_rows + height, :
            ]
            preact = preact + jnp.einsum(
                "ok,kdhw->odhw",
                front_one[along_depth, along_rows],
                window,
                preferred_element_type=jnp.float32,
            )
    hidden = jnp.where(inside, jax.nn.silu(preact), 0.0).astype(jnp.bfloat16)
    stacked = hidden[:, : planes + 1]
    stacked = jnp.pad(stacked, ((0, 0), (0, 0), (1, 1), (0, 0)))
    picks = jnp.arange(columns)[:, None, None] == (
        2 * jnp.arange(half_cols)[None, None, :] + jnp.arange(3)[None, :, None] - 1
    )
    hidden_cols = jnp.einsum(
        "qdhp,pck->cqdhk", stacked, picks.astype(jnp.bfloat16), preferred_element_type=jnp.float32
    )
    hidden_cols = hidden_cols.astype(jnp.bfloat16).reshape(
        3 * channels, planes + 1, height + 2, half_cols
    )
    windows = jnp.stack(
        [
            hidden_cols[
                :,
                along_depth : along_depth + planes - 1 : 2,
                along_rows : along_rows + height - 1 : 2,
                :,
            ]
            for along_depth in range(3)
            for along_rows in range(3)
        ]
    )
    output = jnp.einsum(
        "tok,tkdhw->odhw",
        front_two.reshape(9, channels, 3 * channels),
        windows,
        preferred_element_type=jnp.float32,
    )
    terms_two = jnp.einsum("odhw,tkdhw->tok", cotangent, windows, preferred_element_type=jnp.float32)
    extended = jnp.pad(cot_ext, ((0, 0), (0, 0), (0, 1), (0, 0)))
    spread = jnp.arange(half_cols)[:, None, None] * 2 + jnp.arange(3)[None, :, None] - 1
    spread = (spread == jnp.arange(columns)[None, None, :]).astype(jnp.bfloat16)
    widened = jnp.einsum("odrj,jcw->codrw", extended, spread, preferred_element_type=jnp.float32)
    widened = widened.astype(jnp.bfloat16)
    class_planes = half_planes + 1
    row_taps = [[(1, 0)], [(2, 0), (0, 1)]]
    depth_taps = [[(2, 0), (0, 1)], [(1, 1)]]
    order = []
    for depth_slot in range(2):
        for row_parity in range(2):
            for tap_depth, _ in depth_taps[depth_slot]:
                for tap_row, _ in row_taps[row_parity]:
                    for tap_col in range(3):
                        order.append(9 * tap_depth + 3 * tap_row + tap_col)
    ordered_two = weight_two[np.array(order)]
    taken = 0
    classes = []
    for depth_slot in range(2):
        for row_parity in range(2):
            pieces = []
            for tap_depth, skip_depth in depth_taps[depth_slot]:
                for tap_row, skip_row in row_taps[row_parity]:
                    for tap_col in range(3):
                        pieces.append(
                            widened[
                                tap_col,
                                :,
                                skip_depth : skip_depth + class_planes,
                                skip_row : skip_row + half_rows,
                                :,
                            ]
                        )
            joined = jnp.concatenate(pieces, 0)
            joined_kernel = ordered_two[taken : taken + len(pieces)].reshape(-1, channels)
            taken += len(pieces)
            classes.append(
                jnp.einsum("kq,kdhw->qdhw", joined_kernel, joined, preferred_element_type=jnp.float32)
            )
    parity_grid = jnp.stack(classes).reshape(2, 2, channels, class_planes, half_rows, columns)
    grad_hidden = parity_grid.transpose(2, 3, 0, 4, 1, 5).reshape(
        channels, 2 * class_planes, height, columns
    )
    sigma = jax.nn.sigmoid(preact)
    grad_rim = grad_hidden * (sigma * (1.0 + preact * (1.0 - sigma)))
    grad_rim = jnp.where(inside, grad_rim, 0.0).astype(jnp.bfloat16)
    grad_pre = grad_rim[:, 1 : planes + 1]
    rimmed = pad_sides(grad_rim)
    rimmed_cols = column_stack(rimmed, 1, columns, lambda along_cols: 2 - along_cols)
    grad_volume = jnp.zeros((channels, planes, height, columns), jnp.float32)
    terms_one = []
    for along_depth in range(3):
        for along_rows in range(3):
            window = volume_cols[
                :, along_depth + 1 : along_depth + 1 + planes, along_rows : along_rows + height, :
            ]
            terms_one.append(
                jnp.einsum("odhw,kdhw->ok", grad_pre, window, preferred_element_type=jnp.float32)
            )
            back_window = rimmed_cols[
                :,
                2 - along_depth : 2 - along_depth + planes,
                2 - along_rows : 2 - along_rows + height,
                :,
            ]
            grad_volume = grad_volume + jnp.einsum(
                "qk,kdhw->qdhw",
                rear_one[along_depth, along_rows],
                back_window,
                preferred_element_type=jnp.float32,
            )
    summed = summed_over(jnp.stack([jnp.stack(terms_one), terms_two]), "slab")
    grad_one, grad_two = fold_terms(summed)
    return (output.astype(jnp.bfloat16), grad_volume.astype(jnp.bfloat16), grad_one, grad_two)


def solution(mesh):
    in_specs = (
        P(None, ("grp", "slab"), None, None),
        P(),
        P(),
        P(None, ("grp", "slab"), None, None),
    )
    out_specs = (
        P(None, ("grp", "slab"), None, None),
        P(None, ("grp", "slab"), None, None),
        P("grp", None, None),
        P("grp", None, None),
    )
    return jax.shard_map(
        on_device, mesh=mesh, in_specs=in_specs, out_specs=out_specs, check_vma=False
    )
```

```python
import jax
import numpy as np
import jax.numpy as jnp
from jax import lax
from jax.sharding import PartitionSpec as P


def extended_2(shard, sides, width):
    for axis, dim in sides:
        devices, length = (lax.axis_size(axis), shard.shape[dim])
        up = [(i, (i + 1) % devices) for i in range(devices - 1)]
        down = [(j, i) for i, j in up]
        last = lax.slice_in_dim(shard, length - width, length, axis=dim)
        initial = lax.slice_in_dim(shard, 0, width, axis=dim)
        before = lax.ppermute(last, axis, up)
        after = lax.ppermute(initial, axis, down)
        shard = jnp.concatenate([before, shard, after], axis=dim)
    return shard


def pad_sides(field):
    return jnp.pad(field, ((0, 0), (0, 0), (1, 1), (1, 1)))


def column_stack(field, stride, count, start):
    pieces = []
    for along_cols in range(3):
        first = start(along_cols)
        pieces.append(field[..., first : first + stride * (count - 1) + 1 : stride])
    return jnp.concatenate(pieces, 0)


def summed_over(terms, axis):
    devices = lax.axis_size(axis)
    flat = terms.reshape(-1)
    room = -flat.shape[0] % devices
    flat = jnp.pad(flat, (0, room)).reshape(devices, -1)
    mine = lax.all_to_all(flat, axis, 0, 0, tiled=True).sum(0, keepdims=True)
    whole = lax.all_to_all(jnp.broadcast_to(mine, flat.shape), axis, 0, 0, tiled=True)
    return whole.reshape(-1)[: terms.size].reshape(terms.shape)


def forward_kernel(weights):
    size = weights.shape[1]
    return (
        weights.reshape(3, 3, 3, size, size).transpose(0, 1, 3, 2, 4).reshape(3, 3, size, 3 * size)
    )


def backward_kernel(weights):
    size = weights.shape[1]
    return weights.reshape(3, 3, 3 * size, size)


def fold_terms(summed):
    size = summed.shape[2]
    folded = summed.reshape(2, 9, size, 3, size).transpose(0, 1, 3, 2, 4)
    folded = folded.reshape(2, 27, size, size)
    return folded[0], folded[1]


def layer(volume, weight_one, weight_two, cotangent):
    channels, planes, height, columns = volume.shape
    half_planes = planes // 2
    half_rows = height // 2
    half_cols = columns // 2
    front_one = forward_kernel(weight_one)
    front_two = forward_kernel(weight_two)
    rear_one = backward_kernel(weight_one).transpose(0, 1, 3, 2)
    padded = pad_sides(extended_2(volume, (("slab", 1),), 2))
    volume_cols = column_stack(padded, 1, columns, lambda along_cols: along_cols)
    cot_ext = extended_2(cotangent, (("slab", 1),), 1)
    devices = lax.axis_size("slab")
    place = lax.axis_index("slab") * planes + jnp.arange(-1, planes + 1)
    inside = ((place >= 0) & (place < devices * planes))[None, :, None, None]
    preact = jnp.zeros((channels, planes + 2, height, columns), jnp.float32)
    for along_depth in range(3):
        for along_rows in range(3):
            window = volume_cols[
                :, along_depth : along_depth + planes + 2, along_rows : along_rows + height, :
            ]
            preact = preact + jnp.einsum(
                "ok,kdhw->odhw",
                front_one[along_depth, along_rows],
                window,
                preferred_element_type=jnp.float32,
            )
    hidden = jnp.where(inside, jax.nn.silu(preact), 0.0).astype(jnp.bfloat16)
    stacked = hidden[:, : planes + 1]
    stacked = jnp.pad(stacked, ((0, 0), (0, 0), (1, 1), (0, 0)))
    picks = jnp.arange(columns)[:, None, None] == (
        2 * jnp.arange(half_cols)[None, None, :] + jnp.arange(3)[None, :, None] - 1
    )
    hidden_cols = jnp.einsum(
        "qdhp,pck->cqdhk", stacked, picks.astype(jnp.bfloat16), preferred_element_type=jnp.float32
    )
    hidden_cols = hidden_cols.astype(jnp.bfloat16).reshape(
        3 * channels, planes + 1, height + 2, half_cols
    )
    output = jnp.zeros((channels, half_planes, half_rows, half_cols), jnp.float32)
    terms_two = []
    for along_depth in range(3):
        for along_rows in range(3):
            window = hidden_cols[
                :,
                along_depth : along_depth + planes - 1 : 2,
                along_rows : along_rows + height - 1 : 2,
                :,
            ]
            output = output + jnp.einsum(
                "ok,kdhw->odhw",
                front_two[along_depth, along_rows],
                window,
                preferred_element_type=jnp.float32,
            )
            terms_two.append(
                jnp.einsum("odhw,kdhw->ok", cotangent, window, preferred_element_type=jnp.float32)
            )
    extended = jnp.pad(cot_ext, ((0, 0), (0, 0), (0, 1), (0, 0)))
    spread = jnp.arange(half_cols)[:, None, None] * 2 + jnp.arange(3)[None, :, None] - 1
    spread = (spread == jnp.arange(columns)[None, None, :]).astype(jnp.bfloat16)
    widened = jnp.einsum("odrj,jcw->codrw", extended, spread, preferred_element_type=jnp.float32)
    widened = widened.astype(jnp.bfloat16)
    class_planes = half_planes + 1
    row_taps = [[(1, 0)], [(2, 0), (0, 1)]]
    depth_taps = [[(2, 0), (0, 1)], [(1, 1)]]
    order = []
    for depth_slot in range(2):
        for row_parity in range(2):
            for tap_depth, _ in depth_taps[depth_slot]:
                for tap_row, _ in row_taps[row_parity]:
                    for tap_col in range(3):
                        order.append(9 * tap_depth + 3 * tap_row + tap_col)
    ordered_two = weight_two[np.array(order)]
    taken = 0
    classes = []
    for depth_slot in range(2):
        for row_parity in range(2):
            pieces = []
            for tap_depth, skip_depth in depth_taps[depth_slot]:
                for tap_row, skip_row in row_taps[row_parity]:
                    for tap_col in range(3):
                        pieces.append(
                            widened[
                                tap_col,
                                :,
                                skip_depth : skip_depth + class_planes,
                                skip_row : skip_row + half_rows,
                                :,
                            ]
                        )
            joined = jnp.concatenate(pieces, 0)
            joined_kernel = ordered_two[taken : taken + len(pieces)].reshape(-1, channels)
            taken += len(pieces)
            classes.append(
                jnp.einsum("kq,kdhw->qdhw", joined_kernel, joined, preferred_element_type=jnp.float32)
            )
    parity_grid = jnp.stack(classes).reshape(2, 2, channels, class_planes, half_rows, columns)
    grad_hidden = parity_grid.transpose(2, 3, 0, 4, 1, 5).reshape(
        channels, 2 * class_planes, height, columns
    )
    sigma = jax.nn.sigmoid(preact)
    grad_rim = grad_hidden * (sigma * (1.0 + preact * (1.0 - sigma)))
    grad_rim = jnp.where(inside, grad_rim, 0.0).astype(jnp.bfloat16)
    grad_pre = grad_rim[:, 1 : planes + 1]
    rimmed = pad_sides(grad_rim)
    rimmed_cols = column_stack(rimmed, 1, columns, lambda along_cols: 2 - along_cols)
    grad_volume = jnp.zeros((channels, planes, height, columns), jnp.float32)
    terms_one = []
    for along_depth in range(3):
        for along_rows in range(3):
            window = volume_cols[
                :, along_depth + 1 : along_depth + 1 + planes, along_rows : along_rows + height, :
            ]
            terms_one.append(
                jnp.einsum("odhw,kdhw->ok", grad_pre, window, preferred_element_type=jnp.float32)
            )
            back_window = rimmed_cols[
                :,
                2 - along_depth : 2 - along_depth + planes,
                2 - along_rows : 2 - along_rows + height,
                :,
            ]
            grad_volume = grad_volume + jnp.einsum(
                "qk,kdhw->qdhw",
                rear_one[along_depth, along_rows],
                back_window,
                preferred_element_type=jnp.float32,
            )
    summed = summed_over(jnp.stack([jnp.stack(terms_one), jnp.stack(terms_two)]), "slab")
    grad_one, grad_two = fold_terms(summed)
    return (output.astype(jnp.bfloat16), grad_volume.astype(jnp.bfloat16), grad_one, grad_two)


def solution(mesh):
    in_specs = (
        P(None, ("grp", "slab"), None, None),
        P(),
        P(),
        P(None, ("grp", "slab"), None, None),
    )
    out_specs = (
        P(None, ("grp", "slab"), None, None),
        P(None, ("grp", "slab"), None, None),
        P("grp", None, None),
        P("grp", None, None),
    )
    return jax.shard_map(layer, mesh=mesh, in_specs=in_specs, out_specs=out_specs, check_vma=False)
```

```python
import jax
import numpy as np
import jax.numpy as jnp
from jax import lax
from jax.sharding import PartitionSpec as P


def passed_along(block, axis, distance):
    devices = range(lax.axis_size(axis))
    route = [(i - distance, i) for i in devices if i - distance in devices]
    return lax.ppermute(block, axis, route)


def borders(volume, cotangent, axis):
    channels, planes = volume.shape[:2]
    half_planes = cotangent.shape[1]
    vol_shape = (channels, 2) + volume.shape[2:]
    cot_shape = (channels, 1) + cotangent.shape[2:]
    vol_size = vol_shape[1] * vol_shape[2] * vol_shape[3]
    upward = jnp.concatenate(
        [
            volume[:, planes - 2 :].reshape(channels, -1),
            cotangent[:, half_planes - 1 :].reshape(channels, -1),
        ],
        1,
    )
    downward = jnp.concatenate(
        [volume[:, :2].reshape(channels, -1), cotangent[:, :1].reshape(channels, -1)], 1
    )
    below = passed_along(upward, axis, 1)
    above = passed_along(downward, axis, -1)
    return (
        below[:, :vol_size].reshape(vol_shape),
        above[:, :vol_size].reshape(vol_shape),
        below[:, vol_size:].reshape(cot_shape),
        above[:, vol_size:].reshape(cot_shape),
    )


def pad_sides(field):
    return jnp.pad(field, ((0, 0), (0, 0), (1, 1), (1, 1)))


def column_stack(field, stride, count, start):
    pieces = []
    for along_cols in range(3):
        first = start(along_cols)
        pieces.append(field[..., first : first + stride * (count - 1) + 1 : stride])
    return jnp.concatenate(pieces, 0)


def summed_over(terms, axis):
    devices = lax.axis_size(axis)
    flat = terms.reshape(-1)
    room = -flat.shape[0] % devices
    flat = jnp.pad(flat, (0, room)).reshape(devices, -1)
    mine = lax.all_to_all(flat, axis, 0, 0, tiled=True).sum(0, keepdims=True)
    whole = lax.all_to_all(jnp.broadcast_to(mine, flat.shape), axis, 0, 0, tiled=True)
    return whole.reshape(-1)[: terms.size].reshape(terms.shape)


def forward_kernel(weights):
    size = weights.shape[1]
    return (
        weights.reshape(3, 3, 3, size, size).transpose(0, 1, 3, 2, 4).reshape(3, 3, size, 3 * size)
    )


def backward_kernel(weights):
    size = weights.shape[1]
    return weights.reshape(3, 3, 3 * size, size)


def fold_terms(summed):
    size = summed.shape[2]
    folded = summed.reshape(2, 9, size, 3, size).transpose(0, 1, 3, 2, 4)
    folded = folded.reshape(2, 27, size, size)
    return folded[0], folded[1]


def layer(volume, weight_one, weight_two, cotangent):
    channels, planes, height, columns = volume.shape
    half_planes = planes // 2
    half_rows = height // 2
    half_cols = columns // 2
    front_one = forward_kernel(weight_one)
    front_two = forward_kernel(weight_two)
    rear_one = backward_kernel(weight_one).transpose(0, 1, 3, 2)
    vol_below, vol_above, cot_below, cot_above = borders(volume, cotangent, "slab")
    padded = pad_sides(jnp.concatenate([vol_below, volume, vol_above], 1))
    volume_cols = column_stack(padded, 1, columns, lambda along_cols: along_cols)
    cot_ext = jnp.concatenate([cot_below, cotangent, cot_above], 1)
    devices = lax.axis_size("slab")
    place = lax.axis_index("slab") * planes + jnp.arange(-1, planes + 1)
    inside = ((place >= 0) & (place < devices * planes))[None, :, None, None]
    preact = jnp.zeros((channels, planes + 2, height, columns), jnp.float32)
    for along_depth in range(3):
        for along_rows in range(3):
            window = volume_cols[
                :, along_depth : along_depth + planes + 2, along_rows : along_rows + height, :
            ]
            preact = preact + jnp.einsum(
                "ok,kdhw->odhw",
                front_one[along_depth, along_rows],
                window,
                preferred_element_type=jnp.float32,
            )
    hidden = jnp.where(inside, jax.nn.silu(preact), 0.0).astype(jnp.bfloat16)
    stacked = hidden[:, : planes + 1]
    stacked = jnp.pad(stacked, ((0, 0), (0, 0), (1, 1), (0, 0)))
    picks = jnp.arange(columns)[:, None, None] == (
        2 * jnp.arange(half_cols)[None, None, :] + jnp.arange(3)[None, :, None] - 1
    )
    hidden_cols = jnp.einsum(
        "qdhp,pck->cqdhk", stacked, picks.astype(jnp.bfloat16), preferred_element_type=jnp.float32
    )
    hidden_cols = hidden_cols.astype(jnp.bfloat16).reshape(
        3 * channels, planes + 1, height + 2, half_cols
    )
    output = jnp.zeros((channels, half_planes, half_rows, half_cols), jnp.float32)
    terms_two = []
    for along_depth in range(3):
        for along_rows in range(3):
            window = hidden_cols[
                :,
                along_depth : along_depth + planes - 1 : 2,
                along_rows : along_rows + height - 1 : 2,
                :,
            ]
            output = output + jnp.einsum(
                "ok,kdhw->odhw",
                front_two[along_depth, along_rows],
                window,
                preferred_element_type=jnp.float32,
            )
            terms_two.append(
                jnp.einsum("odhw,kdhw->ok", cotangent, window, preferred_element_type=jnp.float32)
            )
    extended = jnp.pad(cot_ext, ((0, 0), (0, 0), (0, 1), (0, 0)))
    spread = jnp.arange(half_cols)[:, None, None] * 2 + jnp.arange(3)[None, :, None] - 1
    spread = (spread == jnp.arange(columns)[None, None, :]).astype(jnp.bfloat16)
    widened = jnp.einsum("odrj,jcw->codrw", extended, spread, preferred_element_type=jnp.float32)
    widened = widened.astype(jnp.bfloat16)
    class_planes = half_planes + 1
    row_taps = [[(1, 0)], [(2, 0), (0, 1)]]
    depth_taps = [[(2, 0), (0, 1)], [(1, 1)]]
    order = []
    for depth_slot in range(2):
        for row_parity in range(2):
            for tap_depth, _ in depth_taps[depth_slot]:
                for tap_row, _ in row_taps[row_parity]:
                    for tap_col in range(3):
                        order.append(9 * tap_depth + 3 * tap_row + tap_col)
    ordered_two = weight_two[np.array(order)]
    taken = 0
    classes = []
    for depth_slot in range(2):
        for row_parity in range(2):
            pieces = []
            for tap_depth, skip_depth in depth_taps[depth_slot]:
                for tap_row, skip_row in row_taps[row_parity]:
                    for tap_col in range(3):
                        pieces.append(
                            widened[
                                tap_col,
                                :,
                                skip_depth : skip_depth + class_planes,
                                skip_row : skip_row + half_rows,
                                :,
                            ]
                        )
            joined = jnp.concatenate(pieces, 0)
            joined_kernel = ordered_two[taken : taken + len(pieces)].reshape(-1, channels)
            taken += len(pieces)
            classes.append(
                jnp.einsum("kq,kdhw->qdhw", joined_kernel, joined, preferred_element_type=jnp.float32)
            )
    parity_grid = jnp.stack(classes).reshape(2, 2, channels, class_planes, half_rows, columns)
    grad_hidden = parity_grid.transpose(2, 3, 0, 4, 1, 5).reshape(
        channels, 2 * class_planes, height, columns
    )
    sigma = jax.nn.sigmoid(preact)
    grad_rim = grad_hidden * (sigma * (1.0 + preact * (1.0 - sigma)))
    grad_rim = jnp.where(inside, grad_rim, 0.0).astype(jnp.bfloat16)
    grad_pre = grad_rim[:, 1 : planes + 1]
    terms_one = []
    for along_depth in range(3):
        for along_rows in range(3):
            window = volume_cols[
                :, along_depth + 1 : along_depth + 1 + planes, along_rows : along_rows + height, :
            ]
            terms_one.append(
                jnp.einsum("odhw,kdhw->ok", grad_pre, window, preferred_element_type=jnp.float32)
            )
    rimmed = pad_sides(grad_rim)
    rimmed_cols = column_stack(rimmed, 1, columns, lambda along_cols: 2 - along_cols)
    grad_volume = jnp.zeros((channels, planes, height, columns), jnp.float32)
    for along_depth in range(3):
        for along_rows in range(3):
            back_window = rimmed_cols[
                :,
                2 - along_depth : 2 - along_depth + planes,
                2 - along_rows : 2 - along_rows + height,
                :,
            ]
            grad_volume = grad_volume + jnp.einsum(
                "qk,kdhw->qdhw",
                rear_one[along_depth, along_rows],
                back_window,
                preferred_element_type=jnp.float32,
            )
    grad_volume = grad_volume.astype(jnp.bfloat16)
    summed = summed_over(jnp.stack([jnp.stack(terms_one), jnp.stack(terms_two)]), "slab")
    grad_one, grad_two = fold_terms(summed)
    return (output.astype(jnp.bfloat16), grad_volume, grad_one, grad_two)


def solution(mesh):
    in_specs = (
        P(None, ("grp", "slab"), None, None),
        P(),
        P(),
        P(None, ("grp", "slab"), None, None),
    )
    out_specs = (
        P(None, ("grp", "slab"), None, None),
        P(None, ("grp", "slab"), None, None),
        P("grp", None, None),
        P("grp", None, None),
    )
    return jax.shard_map(layer, mesh=mesh, in_specs=in_specs, out_specs=out_specs, check_vma=False)
```

```python
import jax
import numpy as np
import jax.numpy as jnp
from jax import lax
from jax.sharding import PartitionSpec as P


def extended_2(shard, sides, width):
    for axis, dim in sides:
        devices, length = (lax.axis_size(axis), shard.shape[dim])
        up = [(i, (i + 1) % devices) for i in range(devices - 1)]
        down = [(j, i) for i, j in up]
        last = lax.slice_in_dim(shard, length - width, length, axis=dim)
        initial = lax.slice_in_dim(shard, 0, width, axis=dim)
        before = lax.ppermute(last, axis, up)
        after = lax.ppermute(initial, axis, down)
        shard = jnp.concatenate([before, shard, after], axis=dim)
    return shard


def pad_sides(field):
    return jnp.pad(field, ((0, 0), (0, 0), (1, 1), (1, 1)))


def column_stack(field, stride, count, start):
    pieces = []
    for along_cols in range(3):
        first = start(along_cols)
        pieces.append(field[..., first : first + stride * (count - 1) + 1 : stride])
    return jnp.concatenate(pieces, 0)


def summed_over(terms, axis):
    devices = lax.axis_size(axis)
    flat = terms.reshape(-1)
    room = -flat.shape[0] % devices
    flat = jnp.pad(flat, (0, room)).reshape(devices, -1)
    mine = lax.all_to_all(flat, axis, 0, 0, tiled=True).sum(0, keepdims=True)
    whole = lax.all_to_all(jnp.broadcast_to(mine, flat.shape), axis, 0, 0, tiled=True)
    return whole.reshape(-1)[: terms.size].reshape(terms.shape)


def forward_kernel(weights):
    size = weights.shape[1]
    return (
        weights.reshape(3, 3, 3, size, size).transpose(0, 1, 3, 2, 4).reshape(3, 3, size, 3 * size)
    )


def backward_kernel(weights):
    size = weights.shape[1]
    return weights.reshape(3, 3, 3 * size, size)


def fold_terms(summed):
    size = summed.shape[2]
    folded = summed.reshape(2, 9, size, 3, size).transpose(0, 1, 3, 2, 4)
    folded = folded.reshape(2, 27, size, size)
    return folded[0], folded[1]


def layer(volume, weight_one, weight_two, cotangent):
    channels, planes, height, columns = volume.shape
    half_planes = planes // 2
    half_rows = height // 2
    half_cols = columns // 2
    front_one = forward_kernel(weight_one)
    front_two = forward_kernel(weight_two)
    rear_one = backward_kernel(weight_one).transpose(0, 1, 3, 2)
    padded = pad_sides(extended_2(volume, (("slab", 1),), 2))
    volume_cols = column_stack(padded, 1, columns, lambda along_cols: along_cols)
    cot_ext = extended_2(cotangent, (("slab", 1),), 1)
    devices = lax.axis_size("slab")
    place = lax.axis_index("slab") * planes + jnp.arange(-1, planes + 1)
    inside = ((place >= 0) & (place < devices * planes))[None, :, None, None]
    preact = jnp.zeros((channels, planes + 2, height, columns), jnp.float32)
    for along_depth in range(3):
        for along_rows in range(3):
            window = volume_cols[
                :, along_depth : along_depth + planes + 2, along_rows : along_rows + height, :
            ]
            preact = preact + jnp.einsum(
                "ok,kdhw->odhw",
                front_one[along_depth, along_rows],
                window,
                preferred_element_type=jnp.float32,
            )
    hidden = jnp.where(inside, jax.nn.silu(preact), 0.0).astype(jnp.bfloat16)
    stacked = hidden[:, : planes + 1]
    stacked = jnp.pad(stacked, ((0, 0), (0, 0), (1, 1), (0, 0)))
    picks = jnp.arange(columns)[:, None, None] == (
        2 * jnp.arange(half_cols)[None, None, :] + jnp.arange(3)[None, :, None] - 1
    )
    hidden_cols = jnp.einsum(
        "qdhp,pck->cqdhk", stacked, picks.astype(jnp.bfloat16), preferred_element_type=jnp.float32
    )
    hidden_cols = hidden_cols.astype(jnp.bfloat16).reshape(
        3 * channels, planes + 1, height + 2, half_cols
    )
    output = jnp.zeros((channels, half_planes, half_rows, half_cols), jnp.float32)
    terms_two = []
    for along_depth in range(3):
        for along_rows in range(3):
            window = hidden_cols[
                :,
                along_depth : along_depth + planes - 1 : 2,
                along_rows : along_rows + height - 1 : 2,
                :,
            ]
            output = output + jnp.einsum(
                "ok,kdhw->odhw",
                front_two[along_depth, along_rows],
                window,
                preferred_element_type=jnp.float32,
            )
            terms_two.append(
                jnp.einsum("odhw,kdhw->ok", cotangent, window, preferred_element_type=jnp.float32)
            )
    extended = jnp.pad(cot_ext, ((0, 0), (0, 0), (0, 1), (0, 0)))
    spread = jnp.arange(half_cols)[:, None, None] * 2 + jnp.arange(3)[None, :, None] - 1
    spread = (spread == jnp.arange(columns)[None, None, :]).astype(jnp.bfloat16)
    widened = jnp.einsum("odrj,jcw->codrw", extended, spread, preferred_element_type=jnp.float32)
    widened = widened.astype(jnp.bfloat16)
    class_planes = half_planes + 1
    row_taps = [[(1, 0)], [(2, 0), (0, 1)]]
    depth_taps = [[(2, 0), (0, 1)], [(1, 1)]]
    order = []
    for depth_slot in range(2):
        for row_parity in range(2):
            for tap_depth, _ in depth_taps[depth_slot]:
                for tap_row, _ in row_taps[row_parity]:
                    for tap_col in range(3):
                        order.append(9 * tap_depth + 3 * tap_row + tap_col)
    ordered_two = weight_two[np.array(order)]
    taken = 0
    classes = []
    for depth_slot in range(2):
        for row_parity in range(2):
            pieces = []
            for tap_depth, skip_depth in depth_taps[depth_slot]:
                for tap_row, skip_row in row_taps[row_parity]:
                    for tap_col in range(3):
                        pieces.append(
                            widened[
                                tap_col,
                                :,
                                skip_depth : skip_depth + class_planes,
                                skip_row : skip_row + half_rows,
                                :,
                            ]
                        )
            joined = jnp.concatenate(pieces, 0)
            joined_kernel = ordered_two[taken : taken + len(pieces)].reshape(-1, channels)
            taken += len(pieces)
            classes.append(
                jnp.einsum("kq,kdhw->qdhw", joined_kernel, joined, preferred_element_type=jnp.float32)
            )
    parity_grid = jnp.stack(classes).reshape(2, 2, channels, class_planes, half_rows, columns)
    grad_hidden = parity_grid.transpose(2, 3, 0, 4, 1, 5).reshape(
        channels, 2 * class_planes, height, columns
    )
    sigma = jax.nn.sigmoid(preact)
    grad_rim = grad_hidden * (sigma * (1.0 + preact * (1.0 - sigma)))
    grad_rim = jnp.where(inside, grad_rim, 0.0).astype(jnp.bfloat16)
    grad_pre = grad_rim[:, 1 : planes + 1]
    volume_minor = volume_cols[:, 1 : planes + 3].transpose(1, 2, 3, 0)
    terms_one = []
    for along_depth in range(3):
        for along_rows in range(3):
            window = volume_minor[
                along_depth : along_depth + planes, along_rows : along_rows + height
            ]
            terms_one.append(
                jnp.einsum("odhw,dhwk->ok", grad_pre, window, preferred_element_type=jnp.float32)
            )
    rimmed = pad_sides(grad_rim)
    rimmed_cols = column_stack(rimmed, 1, columns, lambda along_cols: 2 - along_cols)
    grad_volume = jnp.zeros((channels, planes, height, columns), jnp.float32)
    for along_depth in range(3):
        for along_rows in range(3):
            back_window = rimmed_cols[
                :,
                2 - along_depth : 2 - along_depth + planes,
                2 - along_rows : 2 - along_rows + height,
                :,
            ]
            grad_volume = grad_volume + jnp.einsum(
                "qk,kdhw->qdhw",
                rear_one[along_depth, along_rows],
                back_window,
                preferred_element_type=jnp.float32,
            )
    grad_volume = grad_volume.astype(jnp.bfloat16)
    summed = summed_over(jnp.stack([jnp.stack(terms_one), jnp.stack(terms_two)]), "slab")
    grad_one, grad_two = fold_terms(summed)
    return (output.astype(jnp.bfloat16), grad_volume, grad_one, grad_two)


def solution(mesh):
    in_specs = (
        P(None, ("grp", "slab"), None, None),
        P(),
        P(),
        P(None, ("grp", "slab"), None, None),
    )
    out_specs = (
        P(None, ("grp", "slab"), None, None),
        P(None, ("grp", "slab"), None, None),
        P("grp", None, None),
        P("grp", None, None),
    )
    return jax.shard_map(layer, mesh=mesh, in_specs=in_specs, out_specs=out_specs, check_vma=False)
```

```python
import jax
import numpy as np
import jax.numpy as jnp
from jax import lax
from jax.sharding import PartitionSpec as P


def extended_2(shard, sides, width):
    for axis, dim in sides:
        devices, length = (lax.axis_size(axis), shard.shape[dim])
        up = [(i, (i + 1) % devices) for i in range(devices - 1)]
        down = [(j, i) for i, j in up]
        last = lax.slice_in_dim(shard, length - width, length, axis=dim)
        initial = lax.slice_in_dim(shard, 0, width, axis=dim)
        before = lax.ppermute(last, axis, up)
        after = lax.ppermute(initial, axis, down)
        shard = jnp.concatenate([before, shard, after], axis=dim)
    return shard


def pad_sides(field):
    return jnp.pad(field, ((0, 0), (0, 0), (1, 1), (1, 1)))


def column_stack(field, stride, count, start):
    pieces = []
    for along_cols in range(3):
        first = start(along_cols)
        pieces.append(field[..., first : first + stride * (count - 1) + 1 : stride])
    return jnp.concatenate(pieces, 0)


def summed_over(terms, axis):
    devices = lax.axis_size(axis)
    width = terms.shape[-1]
    rows = terms.size // width
    lanes = -width % 128
    room = -rows % (8 * devices)
    flat = jnp.pad(terms.reshape(rows, width), ((0, room), (0, lanes)))
    flat = flat.reshape(devices, -1, width + lanes)
    mine = lax.all_to_all(flat, axis, 0, 0).sum(0, keepdims=True)
    whole = lax.all_to_all(jnp.broadcast_to(mine, flat.shape), axis, 0, 0)
    whole = whole.reshape(-1, width + lanes)[:rows, :width]
    return whole.reshape(terms.shape)


def forward_kernel(weights):
    size = weights.shape[1]
    return (
        weights.reshape(3, 3, 3, size, size).transpose(0, 1, 3, 2, 4).reshape(3, 3, size, 3 * size)
    )


def backward_kernel(weights):
    size = weights.shape[1]
    return weights.reshape(3, 3, 3 * size, size)


def fold_terms(summed):
    size = summed.shape[2]
    folded = summed.reshape(2, 9, size, 3, size).transpose(0, 1, 3, 2, 4)
    folded = folded.reshape(2, 27, size, size)
    return folded[0], folded[1]


def layer(volume, weight_one, weight_two, cotangent):
    channels, planes, height, columns = volume.shape
    half_planes = planes // 2
    half_rows = height // 2
    half_cols = columns // 2
    front_one = forward_kernel(weight_one)
    front_two = forward_kernel(weight_two)
    rear_one = backward_kernel(weight_one).transpose(0, 1, 3, 2)
    padded = pad_sides(extended_2(volume, (("slab", 1),), 2))
    volume_cols = column_stack(padded, 1, columns, lambda along_cols: along_cols)
    cot_ext = extended_2(cotangent, (("slab", 1),), 1)
    devices = lax.axis_size("slab")
    place = lax.axis_index("slab") * planes + jnp.arange(-1, planes + 1)
    inside = ((place >= 0) & (place < devices * planes))[None, :, None, None]
    preact = jnp.zeros((channels, planes + 2, height, columns), jnp.float32)
    for along_depth in range(3):
        for along_rows in range(3):
            window = volume_cols[
                :, along_depth : along_depth + planes + 2, along_rows : along_rows + height, :
            ]
            preact = preact + jnp.einsum(
                "ok,kdhw->odhw",
                front_one[along_depth, along_rows],
                window,
                preferred_element_type=jnp.float32,
            )
    hidden = jnp.where(inside, jax.nn.silu(preact), 0.0).astype(jnp.bfloat16)
    stacked = hidden[:, : planes + 1]
    stacked = jnp.pad(stacked, ((0, 0), (0, 0), (1, 1), (0, 0)))
    picks = jnp.arange(columns)[:, None, None] == (
        2 * jnp.arange(half_cols)[None, None, :] + jnp.arange(3)[None, :, None] - 1
    )
    hidden_cols = jnp.einsum(
        "qdhp,pck->cqdhk", stacked, picks.astype(jnp.bfloat16), preferred_element_type=jnp.float32
    )
    hidden_cols = hidden_cols.astype(jnp.bfloat16).reshape(
        3 * channels, planes + 1, height + 2, half_cols
    )
    output = jnp.zeros((channels, half_planes, half_rows, half_cols), jnp.float32)
    terms_two = []
    for along_depth in range(3):
        for along_rows in range(3):
            window = hidden_cols[
                :,
                along_depth : along_depth + planes - 1 : 2,
                along_rows : along_rows + height - 1 : 2,
                :,
            ]
            output = output + jnp.einsum(
                "ok,kdhw->odhw",
                front_two[along_depth, along_rows],
                window,
                preferred_element_type=jnp.float32,
            )
            terms_two.append(
                jnp.einsum("odhw,kdhw->ok", cotangent, window, preferred_element_type=jnp.float32)
            )
    extended = jnp.pad(cot_ext, ((0, 0), (0, 0), (0, 1), (0, 0)))
    spread = jnp.arange(half_cols)[:, None, None] * 2 + jnp.arange(3)[None, :, None] - 1
    spread = (spread == jnp.arange(columns)[None, None, :]).astype(jnp.bfloat16)
    widened = jnp.einsum("odrj,jcw->codrw", extended, spread, preferred_element_type=jnp.float32)
    widened = widened.astype(jnp.bfloat16)
    class_planes = half_planes + 1
    row_taps = [[(1, 0)], [(2, 0), (0, 1)]]
    depth_taps = [[(2, 0), (0, 1)], [(1, 1)]]
    order = []
    for depth_slot in range(2):
        for row_parity in range(2):
            for tap_depth, _ in depth_taps[depth_slot]:
                for tap_row, _ in row_taps[row_parity]:
                    for tap_col in range(3):
                        order.append(9 * tap_depth + 3 * tap_row + tap_col)
    ordered_two = weight_two[np.array(order)]
    taken = 0
    classes = []
    for depth_slot in range(2):
        for row_parity in range(2):
            pieces = []
            for tap_depth, skip_depth in depth_taps[depth_slot]:
                for tap_row, skip_row in row_taps[row_parity]:
                    for tap_col in range(3):
                        pieces.append(
                            widened[
                                tap_col,
                                :,
                                skip_depth : skip_depth + class_planes,
                                skip_row : skip_row + half_rows,
                                :,
                            ]
                        )
            joined = jnp.concatenate(pieces, 0)
            joined_kernel = ordered_two[taken : taken + len(pieces)].reshape(-1, channels)
            taken += len(pieces)
            classes.append(
                jnp.einsum("kq,kdhw->qdhw", joined_kernel, joined, preferred_element_type=jnp.float32)
            )
    parity_grid = jnp.stack(classes).reshape(2, 2, channels, class_planes, half_rows, columns)
    grad_hidden = parity_grid.transpose(2, 3, 0, 4, 1, 5).reshape(
        channels, 2 * class_planes, height, columns
    )
    sigma = jax.nn.sigmoid(preact)
    grad_rim = grad_hidden * (sigma * (1.0 + preact * (1.0 - sigma)))
    grad_rim = jnp.where(inside, grad_rim, 0.0).astype(jnp.bfloat16)
    grad_pre = grad_rim[:, 1 : planes + 1]
    terms_one = []
    for along_depth in range(3):
        for along_rows in range(3):
            window = volume_cols[
                :, along_depth + 1 : along_depth + 1 + planes, along_rows : along_rows + height, :
            ]
            terms_one.append(
                jnp.einsum("odhw,kdhw->ok", grad_pre, window, preferred_element_type=jnp.float32)
            )
    rimmed = pad_sides(grad_rim)
    rimmed_cols = column_stack(rimmed, 1, columns, lambda along_cols: 2 - along_cols)
    grad_volume = jnp.zeros((channels, planes, height, columns), jnp.float32)
    for along_depth in range(3):
        for along_rows in range(3):
            back_window = rimmed_cols[
                :,
                2 - along_depth : 2 - along_depth + planes,
                2 - along_rows : 2 - along_rows + height,
                :,
            ]
            grad_volume = grad_volume + jnp.einsum(
                "qk,kdhw->qdhw",
                rear_one[along_depth, along_rows],
                back_window,
                preferred_element_type=jnp.float32,
            )
    grad_volume = grad_volume.astype(jnp.bfloat16)
    summed = summed_over(jnp.stack([jnp.stack(terms_one), jnp.stack(terms_two)]), "slab")
    grad_one, grad_two = fold_terms(summed)
    return (output.astype(jnp.bfloat16), grad_volume, grad_one, grad_two)


def solution(mesh):
    in_specs = (
        P(None, ("grp", "slab"), None, None),
        P(),
        P(),
        P(None, ("grp", "slab"), None, None),
    )
    out_specs = (
        P(None, ("grp", "slab"), None, None),
        P(None, ("grp", "slab"), None, None),
        P("grp", None, None),
        P("grp", None, None),
    )
    return jax.shard_map(layer, mesh=mesh, in_specs=in_specs, out_specs=out_specs, check_vma=False)
```

```python
import jax
import numpy as np
import jax.numpy as jnp
from jax import lax
from jax.sharding import PartitionSpec as P


def extended_2(shard, sides, width):
    for axis, dim in sides:
        devices, length = (lax.axis_size(axis), shard.shape[dim])
        up = [(i, (i + 1) % devices) for i in range(devices - 1)]
        down = [(j, i) for i, j in up]
        last = lax.slice_in_dim(shard, length - width, length, axis=dim)
        initial = lax.slice_in_dim(shard, 0, width, axis=dim)
        before = lax.ppermute(last, axis, up)
        after = lax.ppermute(initial, axis, down)
        shard = jnp.concatenate([before, shard, after], axis=dim)
    return shard


def pad_sides(field):
    return jnp.pad(field, ((0, 0), (0, 0), (1, 1), (1, 1)))


def column_stack(field, stride, count, start):
    pieces = []
    for along_cols in range(3):
        first = start(along_cols)
        pieces.append(field[..., first : first + stride * (count - 1) + 1 : stride])
    return jnp.concatenate(pieces, 0)


def summed_over(terms, axis):
    devices = lax.axis_size(axis)
    flat = terms.reshape(-1)
    room = -flat.shape[0] % devices
    flat = jnp.pad(flat, (0, room)).reshape(devices, -1)
    mine = lax.all_to_all(flat, axis, 0, 0, tiled=True).sum(0, keepdims=True)
    whole = lax.all_to_all(jnp.broadcast_to(mine, flat.shape), axis, 0, 0, tiled=True)
    return whole.reshape(-1)[: terms.size].reshape(terms.shape)


def forward_kernel(weights):
    size = weights.shape[1]
    return (
        weights.reshape(3, 3, 3, size, size).transpose(0, 1, 3, 2, 4).reshape(3, 3, size, 3 * size)
    )


def backward_kernel(weights):
    size = weights.shape[1]
    return weights.reshape(3, 3, 3 * size, size)


def layer(volume, weight_one, weight_two, cotangent):
    channels, planes, height, columns = volume.shape
    half_planes = planes // 2
    half_rows = height // 2
    half_cols = columns // 2
    front_one = forward_kernel(weight_one)
    front_two = forward_kernel(weight_two)
    rear_one = backward_kernel(weight_one).transpose(0, 1, 3, 2)
    padded = pad_sides(extended_2(volume, (("slab", 1),), 2))
    volume_cols = column_stack(padded, 1, columns, lambda along_cols: along_cols)
    cot_ext = extended_2(cotangent, (("slab", 1),), 1)
    devices = lax.axis_size("slab")
    place = lax.axis_index("slab") * planes + jnp.arange(-1, planes + 1)
    inside = ((place >= 0) & (place < devices * planes))[None, :, None, None]
    preact = jnp.zeros((channels, planes + 2, height, columns), jnp.float32)
    for along_depth in range(3):
        for along_rows in range(3):
            window = volume_cols[
                :, along_depth : along_depth + planes + 2, along_rows : along_rows + height, :
            ]
            preact = preact + jnp.einsum(
                "ok,kdhw->odhw",
                front_one[along_depth, along_rows],
                window,
                preferred_element_type=jnp.float32,
            )
    hidden = jnp.where(inside, jax.nn.silu(preact), 0.0).astype(jnp.bfloat16)
    stacked = hidden[:, : planes + 1]
    stacked = jnp.pad(stacked, ((0, 0), (0, 0), (1, 1), (0, 0)))
    picks = jnp.arange(columns)[:, None, None] == (
        2 * jnp.arange(half_cols)[None, None, :] + jnp.arange(3)[None, :, None] - 1
    )
    hidden_cols = jnp.einsum(
        "qdhp,pck->cqdhk", stacked, picks.astype(jnp.bfloat16), preferred_element_type=jnp.float32
    )
    hidden_cols = hidden_cols.astype(jnp.bfloat16).reshape(
        3 * channels, planes + 1, height + 2, half_cols
    )
    output = jnp.zeros((channels, half_planes, half_rows, half_cols), jnp.float32)
    terms_two = []
    for along_depth in range(3):
        for along_rows in range(3):
            window = hidden_cols[
                :,
                along_depth : along_depth + planes - 1 : 2,
                along_rows : along_rows + height - 1 : 2,
                :,
            ]
            output = output + jnp.einsum(
                "ok,kdhw->odhw",
                front_two[along_depth, along_rows],
                window,
                preferred_element_type=jnp.float32,
            )
            terms_two.append(
                jnp.einsum(
                    "odhw,cqdhw->coq",
                    cotangent,
                    window.reshape((3, channels) + window.shape[1:]),
                    preferred_element_type=jnp.float32,
                )
            )
    extended = jnp.pad(cot_ext, ((0, 0), (0, 0), (0, 1), (0, 0)))
    spread = jnp.arange(half_cols)[:, None, None] * 2 + jnp.arange(3)[None, :, None] - 1
    spread = (spread == jnp.arange(columns)[None, None, :]).astype(jnp.bfloat16)
    widened = jnp.einsum("odrj,jcw->codrw", extended, spread, preferred_element_type=jnp.float32)
    widened = widened.astype(jnp.bfloat16)
    class_planes = half_planes + 1
    row_taps = [[(1, 0)], [(2, 0), (0, 1)]]
    depth_taps = [[(2, 0), (0, 1)], [(1, 1)]]
    order = []
    for depth_slot in range(2):
        for row_parity in range(2):
            for tap_depth, _ in depth_taps[depth_slot]:
                for tap_row, _ in row_taps[row_parity]:
                    for tap_col in range(3):
                        order.append(9 * tap_depth + 3 * tap_row + tap_col)
    ordered_two = weight_two[np.array(order)]
    taken = 0
    classes = []
    for depth_slot in range(2):
        for row_parity in range(2):
            pieces = []
            for tap_depth, skip_depth in depth_taps[depth_slot]:
                for tap_row, skip_row in row_taps[row_parity]:
                    for tap_col in range(3):
                        pieces.append(
                            widened[
                                tap_col,
                                :,
                                skip_depth : skip_depth + class_planes,
                                skip_row : skip_row + half_rows,
                                :,
                            ]
                        )
            joined = jnp.concatenate(pieces, 0)
            joined_kernel = ordered_two[taken : taken + len(pieces)].reshape(-1, channels)
            taken += len(pieces)
            classes.append(
                jnp.einsum("kq,kdhw->qdhw", joined_kernel, joined, preferred_element_type=jnp.float32)
            )
    parity_grid = jnp.stack(classes).reshape(2, 2, channels, class_planes, half_rows, columns)
    grad_hidden = parity_grid.transpose(2, 3, 0, 4, 1, 5).reshape(
        channels, 2 * class_planes, height, columns
    )
    sigma = jax.nn.sigmoid(preact)
    grad_rim = grad_hidden * (sigma * (1.0 + preact * (1.0 - sigma)))
    grad_rim = jnp.where(inside, grad_rim, 0.0).astype(jnp.bfloat16)
    grad_pre = grad_rim[:, 1 : planes + 1]
    terms_one = []
    for along_depth in range(3):
        for along_rows in range(3):
            window = volume_cols[
                :, along_depth + 1 : along_depth + 1 + planes, along_rows : along_rows + height, :
            ]
            terms_one.append(
                jnp.einsum(
                    "odhw,cqdhw->coq",
                    grad_pre,
                    window.reshape((3, channels) + window.shape[1:]),
                    preferred_element_type=jnp.float32,
                )
            )
    rimmed = pad_sides(grad_rim)
    rimmed_cols = column_stack(rimmed, 1, columns, lambda along_cols: 2 - along_cols)
    grad_volume = jnp.zeros((channels, planes, height, columns), jnp.float32)
    for along_depth in range(3):
        for along_rows in range(3):
            back_window = rimmed_cols[
                :,
                2 - along_depth : 2 - along_depth + planes,
                2 - along_rows : 2 - along_rows + height,
                :,
            ]
            grad_volume = grad_volume + jnp.einsum(
                "qk,kdhw->qdhw",
                rear_one[along_depth, along_rows],
                back_window,
                preferred_element_type=jnp.float32,
            )
    grad_volume = grad_volume.astype(jnp.bfloat16)
    summed = summed_over(jnp.stack([jnp.stack(terms_one), jnp.stack(terms_two)]), "slab")
    folded = summed.reshape(2, 27, channels, channels)
    grad_one, grad_two = folded[0], folded[1]
    return (output.astype(jnp.bfloat16), grad_volume, grad_one, grad_two)


def solution(mesh):
    in_specs = (
        P(None, ("grp", "slab"), None, None),
        P(),
        P(),
        P(None, ("grp", "slab"), None, None),
    )
    out_specs = (
        P(None, ("grp", "slab"), None, None),
        P(None, ("grp", "slab"), None, None),
        P("grp", None, None),
        P("grp", None, None),
    )
    return jax.shard_map(layer, mesh=mesh, in_specs=in_specs, out_specs=out_specs, check_vma=False)
```

```python
import jax
import numpy as np
import jax.numpy as jnp
from jax import lax
from jax.sharding import PartitionSpec as P


def extended_2(shard, sides, width):
    for axis, dim in sides:
        devices, length = (lax.axis_size(axis), shard.shape[dim])
        up = [(i, (i + 1) % devices) for i in range(devices - 1)]
        down = [(j, i) for i, j in up]
        last = lax.slice_in_dim(shard, length - width, length, axis=dim)
        initial = lax.slice_in_dim(shard, 0, width, axis=dim)
        before = lax.ppermute(last, axis, up)
        after = lax.ppermute(initial, axis, down)
        shard = jnp.concatenate([before, shard, after], axis=dim)
    return shard


def pad_sides(field):
    return jnp.pad(field, ((0, 0), (0, 0), (1, 1), (1, 1)))


def column_stack(field, stride, count, start):
    pieces = []
    for along_cols in range(3):
        first = start(along_cols)
        pieces.append(field[..., first : first + stride * (count - 1) + 1 : stride])
    return jnp.concatenate(pieces, 0)


def summed_over(terms, axis):
    devices = lax.axis_size(axis)
    flat = terms.reshape(-1)
    room = -flat.shape[0] % (devices * 128)
    flat = jnp.pad(flat, (0, room)).reshape(devices, -1, 128)
    mine = lax.all_to_all(flat, axis, 0, 0).sum(0, keepdims=True)
    whole = lax.all_to_all(jnp.broadcast_to(mine, flat.shape), axis, 0, 0)
    return whole.reshape(-1)[: terms.size].reshape(terms.shape)


def forward_kernel(weights):
    size = weights.shape[1]
    return (
        weights.reshape(3, 3, 3, size, size).transpose(0, 1, 3, 2, 4).reshape(3, 3, size, 3 * size)
    )


def backward_kernel(weights):
    size = weights.shape[1]
    return weights.reshape(3, 3, 3 * size, size)


def fold_terms(summed):
    size = summed.shape[2]
    folded = summed.reshape(2, 9, size, 3, size).transpose(0, 1, 3, 2, 4)
    folded = folded.reshape(2, 27, size, size)
    return folded[0], folded[1]


def layer(volume, weight_one, weight_two, cotangent):
    channels, planes, height, columns = volume.shape
    half_planes = planes // 2
    half_rows = height // 2
    half_cols = columns // 2
    front_one = forward_kernel(weight_one)
    front_two = forward_kernel(weight_two)
    rear_one = backward_kernel(weight_one).transpose(0, 1, 3, 2)
    padded = pad_sides(extended_2(volume, (("slab", 1),), 2))
    volume_cols = column_stack(padded, 1, columns, lambda along_cols: along_cols)
    cot_ext = extended_2(cotangent, (("slab", 1),), 1)
    devices = lax.axis_size("slab")
    place = lax.axis_index("slab") * planes + jnp.arange(-1, planes + 1)
    inside = ((place >= 0) & (place < devices * planes))[None, :, None, None]
    preact = jnp.zeros((channels, planes + 2, height, columns), jnp.float32)
    for along_depth in range(3):
        for along_rows in range(3):
            window = volume_cols[
                :, along_depth : along_depth + planes + 2, along_rows : along_rows + height, :
            ]
            preact = preact + jnp.einsum(
                "ok,kdhw->odhw",
                front_one[along_depth, along_rows],
                window,
                preferred_element_type=jnp.float32,
            )
    hidden = jnp.where(inside, jax.nn.silu(preact), 0.0).astype(jnp.bfloat16)
    stacked = hidden[:, : planes + 1]
    stacked = jnp.pad(stacked, ((0, 0), (0, 0), (1, 1), (0, 0)))
    picks = jnp.arange(columns)[:, None, None] == (
        2 * jnp.arange(half_cols)[None, None, :] + jnp.arange(3)[None, :, None] - 1
    )
    hidden_cols = jnp.einsum(
        "qdhp,pck->cqdhk", stacked, picks.astype(jnp.bfloat16), preferred_element_type=jnp.float32
    )
    hidden_cols = hidden_cols.astype(jnp.bfloat16).reshape(
        3 * channels, planes + 1, height + 2, half_cols
    )
    output = jnp.zeros((channels, half_planes, half_rows, half_cols), jnp.float32)
    terms_two = []
    for along_depth in range(3):
        for along_rows in range(3):
            window = hidden_cols[
                :,
                along_depth : along_depth + planes - 1 : 2,
                along_rows : along_rows + height - 1 : 2,
                :,
            ]
            output = output + jnp.einsum(
                "ok,kdhw->odhw",
                front_two[along_depth, along_rows],
                window,
                preferred_element_type=jnp.float32,
            )
            terms_two.append(
                jnp.einsum("odhw,kdhw->ok", cotangent, window, preferred_element_type=jnp.float32)
            )
    extended = jnp.pad(cot_ext, ((0, 0), (0, 0), (0, 1), (0, 0)))
    spread = jnp.arange(half_cols)[:, None, None] * 2 + jnp.arange(3)[None, :, None] - 1
    spread = (spread == jnp.arange(columns)[None, None, :]).astype(jnp.bfloat16)
    widened = jnp.einsum("odrj,jcw->codrw", extended, spread, preferred_element_type=jnp.float32)
    widened = widened.astype(jnp.bfloat16)
    class_planes = half_planes + 1
    row_taps = [[(1, 0)], [(2, 0), (0, 1)]]
    depth_taps = [[(2, 0), (0, 1)], [(1, 1)]]
    order = []
    for depth_slot in range(2):
        for row_parity in range(2):
            for tap_depth, _ in depth_taps[depth_slot]:
                for tap_row, _ in row_taps[row_parity]:
                    for tap_col in range(3):
                        order.append(9 * tap_depth + 3 * tap_row + tap_col)
    ordered_two = weight_two[np.array(order)]
    taken = 0
    classes = []
    for depth_slot in range(2):
        for row_parity in range(2):
            pieces = []
            for tap_depth, skip_depth in depth_taps[depth_slot]:
                for tap_row, skip_row in row_taps[row_parity]:
                    for tap_col in range(3):
                        pieces.append(
                            widened[
                                tap_col,
                                :,
                                skip_depth : skip_depth + class_planes,
                                skip_row : skip_row + half_rows,
                                :,
                            ]
                        )
            joined = jnp.concatenate(pieces, 0)
            joined_kernel = ordered_two[taken : taken + len(pieces)].reshape(-1, channels)
            taken += len(pieces)
            classes.append(
                jnp.einsum("kq,kdhw->qdhw", joined_kernel, joined, preferred_element_type=jnp.float32)
            )
    parity_grid = jnp.stack(classes).reshape(2, 2, channels, class_planes, half_rows, columns)
    grad_hidden = parity_grid.transpose(2, 3, 0, 4, 1, 5).reshape(
        channels, 2 * class_planes, height, columns
    )
    sigma = jax.nn.sigmoid(preact)
    grad_rim = grad_hidden * (sigma * (1.0 + preact * (1.0 - sigma)))
    grad_rim = jnp.where(inside, grad_rim, 0.0).astype(jnp.bfloat16)
    grad_pre = grad_rim[:, 1 : planes + 1]
    terms_one = []
    for along_depth in range(3):
        for along_rows in range(3):
            window = volume_cols[
                :, along_depth + 1 : along_depth + 1 + planes, along_rows : along_rows + height, :
            ]
            terms_one.append(
                jnp.einsum("odhw,kdhw->ok", grad_pre, window, preferred_element_type=jnp.float32)
            )
    rimmed = pad_sides(grad_rim)
    rimmed_cols = column_stack(rimmed, 1, columns, lambda along_cols: 2 - along_cols)
    grad_volume = jnp.zeros((channels, planes, height, columns), jnp.float32)
    for along_depth in range(3):
        for along_rows in range(3):
            back_window = rimmed_cols[
                :,
                2 - along_depth : 2 - along_depth + planes,
                2 - along_rows : 2 - along_rows + height,
                :,
            ]
            grad_volume = grad_volume + jnp.einsum(
                "qk,kdhw->qdhw",
                rear_one[along_depth, along_rows],
                back_window,
                preferred_element_type=jnp.float32,
            )
    grad_volume = grad_volume.astype(jnp.bfloat16)
    summed = summed_over(jnp.stack([jnp.stack(terms_one), jnp.stack(terms_two)]), "slab")
    grad_one, grad_two = fold_terms(summed)
    return (output.astype(jnp.bfloat16), grad_volume, grad_one, grad_two)


def solution(mesh):
    in_specs = (
        P(None, ("grp", "slab"), None, None),
        P(),
        P(),
        P(None, ("grp", "slab"), None, None),
    )
    out_specs = (
        P(None, ("grp", "slab"), None, None),
        P(None, ("grp", "slab"), None, None),
        P("grp", None, None),
        P("grp", None, None),
    )
    return jax.shard_map(layer, mesh=mesh, in_specs=in_specs, out_specs=out_specs, check_vma=False)
```

```python
import jax
import numpy as np
import jax.numpy as jnp
from jax import lax
from jax.sharding import PartitionSpec as P


def extended_2(shard, sides, width):
    for axis, dim in sides:
        devices, length = (lax.axis_size(axis), shard.shape[dim])
        up = [(i, (i + 1) % devices) for i in range(devices - 1)]
        down = [(j, i) for i, j in up]
        last = lax.slice_in_dim(shard, length - width, length, axis=dim)
        initial = lax.slice_in_dim(shard, 0, width, axis=dim)
        before = lax.ppermute(last, axis, up)
        after = lax.ppermute(initial, axis, down)
        shard = jnp.concatenate([before, shard, after], axis=dim)
    return shard


def pad_sides(field):
    return jnp.pad(field, ((0, 0), (0, 0), (1, 1), (1, 1)))


def column_stack(field, stride, count, start):
    pieces = []
    for along_cols in range(3):
        first = start(along_cols)
        pieces.append(field[..., first : first + stride * (count - 1) + 1 : stride])
    return jnp.concatenate(pieces, 0)


def summed_over(terms, axis):
    devices = lax.axis_size(axis)
    flat = terms.reshape(-1)
    room = -flat.shape[0] % devices
    flat = jnp.pad(flat, (0, room)).reshape(devices, -1)
    mine = lax.all_to_all(flat, axis, 0, 0, tiled=True).sum(0, keepdims=True)
    whole = lax.all_to_all(jnp.broadcast_to(mine, flat.shape), axis, 0, 0, tiled=True)
    return whole.reshape(-1)[: terms.size].reshape(terms.shape)


def forward_kernel(weights):
    size = weights.shape[1]
    return (
        weights.reshape(3, 3, 3, size, size).transpose(0, 1, 3, 2, 4).reshape(3, 3, size, 3 * size)
    )


def backward_kernel(weights):
    size = weights.shape[1]
    return weights.reshape(3, 3, 3 * size, size)


def fold_terms(summed):
    size = summed.shape[2]
    folded = summed.reshape(2, 9, size, 3, size).transpose(0, 1, 3, 2, 4)
    folded = folded.reshape(2, 27, size, size)
    return folded[0], folded[1]


def layer(volume, weight_one, weight_two, cotangent):
    channels, planes, height, columns = volume.shape
    half_planes = planes // 2
    half_rows = height // 2
    half_cols = columns // 2
    front_one = forward_kernel(weight_one)
    front_two = forward_kernel(weight_two)
    rear_one = backward_kernel(weight_one).transpose(0, 1, 3, 2)
    padded = pad_sides(extended_2(volume, (("slab", 1),), 2))
    volume_cols = column_stack(padded, 1, columns, lambda along_cols: along_cols)
    cot_ext = extended_2(cotangent, (("slab", 1),), 1)
    devices = lax.axis_size("slab")
    place = lax.axis_index("slab") * planes + jnp.arange(-1, planes + 1)
    inside = ((place >= 0) & (place < devices * planes))[None, :, None, None]
    preact = jnp.zeros((channels, planes + 2, height, columns), jnp.float32)
    for along_depth in range(3):
        for along_rows in range(3):
            window = volume_cols[
                :, along_depth : along_depth + planes + 2, along_rows : along_rows + height, :
            ]
            preact = preact + jnp.einsum(
                "ok,kdhw->odhw",
                front_one[along_depth, along_rows],
                window,
                preferred_element_type=jnp.float32,
            )
    hidden = jnp.where(inside, jax.nn.silu(preact), 0.0).astype(jnp.bfloat16)
    stacked = hidden[:, : planes + 1]
    stacked = jnp.pad(stacked, ((0, 0), (0, 0), (1, 1), (0, 0)))
    picks = jnp.arange(columns)[:, None, None] == (
        2 * jnp.arange(half_cols)[None, None, :] + jnp.arange(3)[None, :, None] - 1
    )
    hidden_cols = jnp.einsum(
        "qdhp,pck->cqdhk", stacked, picks.astype(jnp.bfloat16), preferred_element_type=jnp.float32
    )
    hidden_cols = hidden_cols.astype(jnp.bfloat16).reshape(
        3 * channels, planes + 1, height + 2, half_cols
    )
    output = jnp.zeros((channels, half_planes, half_rows, half_cols), jnp.float32)
    terms_two = []
    for along_depth in range(3):
        for along_rows in range(3):
            window = hidden_cols[
                :,
                along_depth : along_depth + planes - 1 : 2,
                along_rows : along_rows + height - 1 : 2,
                :,
            ]
            output = output + jnp.einsum(
                "ok,kdhw->odhw",
                front_two[along_depth, along_rows],
                window,
                preferred_element_type=jnp.float32,
            )
            terms_two.append(
                jnp.einsum("odhw,kdhw->ok", cotangent, window, preferred_element_type=jnp.float32)
            )
    extended = jnp.pad(cot_ext, ((0, 0), (0, 0), (0, 1), (0, 0)))
    spread = jnp.arange(half_cols)[:, None, None] * 2 + jnp.arange(3)[None, :, None] - 1
    spread = (spread == jnp.arange(columns)[None, None, :]).astype(jnp.bfloat16)
    widened = jnp.einsum("odrj,jcw->codrw", extended, spread, preferred_element_type=jnp.float32)
    widened = widened.astype(jnp.bfloat16)
    class_planes = half_planes + 1
    row_taps = [[(1, 0)], [(2, 0), (0, 1)]]
    depth_taps = [[(2, 0), (0, 1)], [(1, 1)]]
    order = []
    for depth_slot in range(2):
        for row_parity in range(2):
            for tap_depth, _ in depth_taps[depth_slot]:
                for tap_row, _ in row_taps[row_parity]:
                    for tap_col in range(3):
                        order.append(9 * tap_depth + 3 * tap_row + tap_col)
    ordered_two = weight_two[np.array(order)]
    taken = 0
    classes = []
    for depth_slot in range(2):
        for row_parity in range(2):
            pieces = []
            for tap_depth, skip_depth in depth_taps[depth_slot]:
                for tap_row, skip_row in row_taps[row_parity]:
                    for tap_col in range(3):
                        pieces.append(
                            widened[
                                tap_col,
                                :,
                                skip_depth : skip_depth + class_planes,
                                skip_row : skip_row + half_rows,
                                :,
                            ]
                        )
            joined = jnp.concatenate(pieces, 0)
            joined_kernel = ordered_two[taken : taken + len(pieces)].reshape(-1, channels)
            taken += len(pieces)
            classes.append(
                jnp.einsum("kq,kdhw->qdhw", joined_kernel, joined, preferred_element_type=jnp.float32)
            )
    parity_grid = jnp.stack(classes).reshape(2, 2, channels, class_planes, half_rows, columns)
    grad_hidden = parity_grid.transpose(2, 3, 0, 4, 1, 5).reshape(
        channels, 2 * class_planes, height, columns
    )
    sigma = jax.nn.sigmoid(preact)
    grad_rim = grad_hidden * (sigma * (1.0 + preact * (1.0 - sigma)))
    grad_rim = jnp.where(inside, grad_rim, 0.0).astype(jnp.bfloat16)
    grad_pre = grad_rim[:, 1 : planes + 1]
    terms_one = []
    for along_depth in range(3):
        for along_rows in range(3):
            window = volume_cols[
                :, along_depth + 1 : along_depth + 1 + planes, along_rows : along_rows + height, :
            ]
            terms_one.append(
                jnp.einsum("odhw,kdhw->ok", grad_pre, window, preferred_element_type=jnp.float32)
            )
    rimmed = pad_sides(grad_rim)
    rimmed_cols = column_stack(rimmed, 1, columns, lambda along_cols: 2 - along_cols)
    grad_volume = jnp.zeros((channels, planes, height, columns), jnp.float32)
    for along_depth in range(3):
        for along_rows in range(3):
            back_window = rimmed_cols[
                :,
                2 - along_depth : 2 - along_depth + planes,
                2 - along_rows : 2 - along_rows + height,
                :,
            ]
            grad_volume = grad_volume + jnp.einsum(
                "qk,kdhw->qdhw",
                rear_one[along_depth, along_rows],
                back_window,
                preferred_element_type=jnp.float32,
            )
    grad_volume = grad_volume.astype(jnp.bfloat16)
    summed = summed_over(jnp.stack([jnp.stack(terms_one), jnp.stack(terms_two)]), "slab")
    grad_one, grad_two = fold_terms(summed)
    return (output.astype(jnp.bfloat16), grad_volume, grad_one, grad_two)


def solution(mesh):
    in_specs = (
        P(None, ("grp", "slab"), None, None),
        P(),
        P(),
        P(None, ("grp", "slab"), None, None),
    )
    out_specs = (
        P(None, ("grp", "slab"), None, None),
        P(None, ("grp", "slab"), None, None),
        P("grp", None, None),
        P("grp", None, None),
    )
    return jax.shard_map(layer, mesh=mesh, in_specs=in_specs, out_specs=out_specs, check_vma=False)
```

```python
import jax
import jax.numpy as jnp
from jax import lax
from jax.sharding import PartitionSpec as P


def extended_2(shard, sides, width):
    for axis, dim in sides:
        devices, length = (lax.axis_size(axis), shard.shape[dim])
        up = [(i, (i + 1) % devices) for i in range(devices - 1)]
        down = [(j, i) for i, j in up]
        last = lax.slice_in_dim(shard, length - width, length, axis=dim)
        initial = lax.slice_in_dim(shard, 0, width, axis=dim)
        before = lax.ppermute(last, axis, up)
        after = lax.ppermute(initial, axis, down)
        shard = jnp.concatenate([before, shard, after], axis=dim)
    return shard


def pad_sides(field):
    return jnp.pad(field, ((0, 0), (0, 0), (1, 1), (1, 1)))


def column_stack(field, stride, count, start):
    pieces = []
    for along_cols in range(3):
        first = start(along_cols)
        pieces.append(field[..., first : first + stride * (count - 1) + 1 : stride])
    return jnp.concatenate(pieces, 0)


def summed_over(terms, axis):
    devices = lax.axis_size(axis)
    flat = terms.reshape(-1)
    room = -flat.shape[0] % devices
    flat = jnp.pad(flat, (0, room)).reshape(devices, -1)
    mine = lax.all_to_all(flat, axis, 0, 0, tiled=True).sum(0, keepdims=True)
    whole = lax.all_to_all(jnp.broadcast_to(mine, flat.shape), axis, 0, 0, tiled=True)
    return whole.reshape(-1)[: terms.size].reshape(terms.shape)


def forward_kernel(weights):
    size = weights.shape[1]
    return (
        weights.reshape(3, 3, 3, size, size).transpose(0, 1, 3, 2, 4).reshape(3, 3, size, 3 * size)
    )


def backward_kernel(weights):
    size = weights.shape[1]
    return weights.reshape(3, 3, 3 * size, size)


def fold_terms(summed):
    size = summed.shape[2]
    folded = summed.reshape(2, 9, size, 3, size).transpose(0, 1, 3, 2, 4)
    folded = folded.reshape(2, 27, size, size)
    return folded[0], folded[1]


def layer(volume, weight_one, weight_two, cotangent):
    channels, planes, height, columns = volume.shape
    half_planes = planes // 2
    half_rows = height // 2
    half_cols = columns // 2
    front_one = forward_kernel(weight_one)
    front_two = forward_kernel(weight_two)
    rear_one = backward_kernel(weight_one).transpose(0, 1, 3, 2)
    padded = pad_sides(extended_2(volume, (("slab", 1),), 2))
    volume_cols = column_stack(padded, 1, columns, lambda along_cols: along_cols)
    cot_ext = extended_2(cotangent, (("slab", 1),), 1)
    devices = lax.axis_size("slab")
    place = lax.axis_index("slab") * planes + jnp.arange(-1, planes + 1)
    inside = ((place >= 0) & (place < devices * planes))[None, :, None, None]
    preact = jnp.zeros((channels, planes + 2, height, columns), jnp.float32)
    for along_depth in range(3):
        for along_rows in range(3):
            window = volume_cols[
                :, along_depth : along_depth + planes + 2, along_rows : along_rows + height, :
            ]
            preact = preact + jnp.einsum(
                "ok,kdhw->odhw",
                front_one[along_depth, along_rows],
                window,
                preferred_element_type=jnp.float32,
            )
    hidden = jnp.where(inside, jax.nn.silu(preact), 0.0).astype(jnp.bfloat16)
    stacked = hidden[:, : planes + 1]
    stacked = jnp.pad(stacked, ((0, 0), (0, 0), (1, 1), (0, 0)))
    picks = jnp.arange(columns)[:, None, None] == (
        2 * jnp.arange(half_cols)[None, None, :] + jnp.arange(3)[None, :, None] - 1
    )
    hidden_cols = jnp.einsum(
        "qdhp,pck->cqdhk", stacked, picks.astype(jnp.bfloat16), preferred_element_type=jnp.float32
    )
    hidden_cols = hidden_cols.astype(jnp.bfloat16).reshape(
        3 * channels, planes + 1, height + 2, half_cols
    )
    output = jnp.zeros((channels, half_planes, half_rows, half_cols), jnp.float32)
    terms_two = []
    for along_depth in range(3):
        for along_rows in range(3):
            window = hidden_cols[
                :,
                along_depth : along_depth + planes - 1 : 2,
                along_rows : along_rows + height - 1 : 2,
                :,
            ]
            output = output + jnp.einsum(
                "ok,kdhw->odhw",
                front_two[along_depth, along_rows],
                window,
                preferred_element_type=jnp.float32,
            )
            terms_two.append(
                jnp.einsum("odhw,kdhw->ok", cotangent, window, preferred_element_type=jnp.float32)
            )
    extended = jnp.pad(cot_ext, ((0, 0), (0, 0), (0, 1), (0, 0)))
    spread = jnp.arange(half_cols)[:, None, None] * 2 + jnp.arange(3)[None, :, None] - 1
    spread = (spread == jnp.arange(columns)[None, None, :]).astype(jnp.bfloat16)
    widened = jnp.einsum("odrj,jcw->codrw", extended, spread, preferred_element_type=jnp.float32)
    widened = widened.astype(jnp.bfloat16)
    class_planes = half_planes + 1
    row_taps = [[(1, 0)], [(2, 0), (0, 1)]]
    depth_taps = [[(2, 0), (0, 1)], [(1, 1)]]
    order = []
    for depth_slot in range(2):
        for row_parity in range(2):
            for tap_depth, _ in depth_taps[depth_slot]:
                for tap_row, _ in row_taps[row_parity]:
                    for tap_col in range(3):
                        order.append(9 * tap_depth + 3 * tap_row + tap_col)
    ordered_two = jnp.concatenate([weight_two[tap : tap + 1] for tap in order], 0)
    taken = 0
    classes = []
    for depth_slot in range(2):
        for row_parity in range(2):
            pieces = []
            for tap_depth, skip_depth in depth_taps[depth_slot]:
                for tap_row, skip_row in row_taps[row_parity]:
                    for tap_col in range(3):
                        pieces.append(
                            widened[
                                tap_col,
                                :,
                                skip_depth : skip_depth + class_planes,
                                skip_row : skip_row + half_rows,
                                :,
                            ]
                        )
            joined = jnp.concatenate(pieces, 0)
            joined_kernel = ordered_two[taken : taken + len(pieces)].reshape(-1, channels)
            taken += len(pieces)
            classes.append(
                jnp.einsum("kq,kdhw->qdhw", joined_kernel, joined, preferred_element_type=jnp.float32)
            )
    parity_grid = jnp.stack(classes).reshape(2, 2, channels, class_planes, half_rows, columns)
    grad_hidden = parity_grid.transpose(2, 3, 0, 4, 1, 5).reshape(
        channels, 2 * class_planes, height, columns
    )
    sigma = jax.nn.sigmoid(preact)
    grad_rim = grad_hidden * (sigma * (1.0 + preact * (1.0 - sigma)))
    grad_rim = jnp.where(inside, grad_rim, 0.0).astype(jnp.bfloat16)
    grad_pre = grad_rim[:, 1 : planes + 1]
    terms_one = []
    for along_depth in range(3):
        for along_rows in range(3):
            window = volume_cols[
                :, along_depth + 1 : along_depth + 1 + planes, along_rows : along_rows + height, :
            ]
            terms_one.append(
                jnp.einsum("odhw,kdhw->ok", grad_pre, window, preferred_element_type=jnp.float32)
            )
    rimmed = pad_sides(grad_rim)
    rimmed_cols = column_stack(rimmed, 1, columns, lambda along_cols: 2 - along_cols)
    grad_volume = jnp.zeros((channels, planes, height, columns), jnp.float32)
    for along_depth in range(3):
        for along_rows in range(3):
            back_window = rimmed_cols[
                :,
                2 - along_depth : 2 - along_depth + planes,
                2 - along_rows : 2 - along_rows + height,
                :,
            ]
            grad_volume = grad_volume + jnp.einsum(
                "qk,kdhw->qdhw",
                rear_one[along_depth, along_rows],
                back_window,
                preferred_element_type=jnp.float32,
            )
    grad_volume = grad_volume.astype(jnp.bfloat16)
    stacked_terms = jnp.stack(terms_one + terms_two).reshape((2, 9) + terms_one[0].shape)
    summed = summed_over(stacked_terms, "slab")
    grad_one, grad_two = fold_terms(summed)
    return (output.astype(jnp.bfloat16), grad_volume, grad_one, grad_two)


def solution(mesh):
    in_specs = (
        P(None, ("grp", "slab"), None, None),
        P(),
        P(),
        P(None, ("grp", "slab"), None, None),
    )
    out_specs = (
        P(None, ("grp", "slab"), None, None),
        P(None, ("grp", "slab"), None, None),
        P("grp", None, None),
        P("grp", None, None),
    )
    return jax.shard_map(layer, mesh=mesh, in_specs=in_specs, out_specs=out_specs, check_vma=False)
```
